32 devices in a mesh: tm: 8 (over z, x), height: 2 (over core), batch: 2 (over y).
Axes of the slice: x: 2, y: 2, z: 4, core: 2. Of those that a mesh axis runs over, the one named last changes fastest.
Arguments:
- inputs: float32 [2, 32, 4, 160, 96], P('batch', 'tm', 'height'), may hold values from -6 to 6
- weight_one: float32 [3, 3, 3, 96, 96], replicated, may hold values from -0.125 to 0.125
- bias_one: float32 [96], replicated, may hold values from -4 to 4
- gain_one: float32 [96], replicated, may hold values from 0.25 to 1.75
- weight_two: float32 [3, 3, 3, 96, 96], replicated, may hold values from -0.125 to 0.125
- gain_two: float32 [96], replicated, may hold values from 0.25 to 1.75
- cotangent: float32 [2, 32, 4, 160, 96], P('batch', 'tm', 'height'), may hold values from -6 to 6
Outputs:
- grad_inputs: float32 [2, 32, 4, 160, 96], P('batch', 'tm', 'height')
- grad_weight_one: float32 [2592, 96], P('tm')
- grad_weight_two: float32 [2592, 96], P('tm')
- grad_vectors: float32 [4, 96], replicated
The draws below stay inside these ranges and needn't reach their ends.
All inputs are finite; a program needn't handle non-finite values.
Results may differ from the reference program's by a relative error of at most 0.00012.
Values sent between devices are 32-bit elements; how exact they have to be, the bound alone decides.
No kernel may reach another device: no remote copies, remote signals or barrier semaphores. Data moves between devices by JAX's collectives and lax.ppermute only.
A program may use at most 128 MiB of HBM per device.

```python
import math
import jax
import jax.numpy as jnp
from jax import lax

C = 96
W = 160
FRAMES = 32
ROWS = 4
CLIPS = 2


def levels(key, shape, split, low, largest):
    level, own = 1.0, jax.random.fold_in(key, 6)
    for position, blocks in split:
        draws = jnp.exp(jax.random.uniform(jax.random.fold_in(own, position), (blocks,), jnp.float32, low / len(split), largest / len(split)))
        level = level * jnp.repeat(draws, shape[position] // blocks).reshape([-1 if axis == position else 1 for axis in range(len(shape))])
    return level


def normal_values(rng, shape, scale, bound, shards=(), kind=jnp.bfloat16):
    values = jax.random.normal(rng, shape, jnp.float32) * scale
    if len(shards) > 0:
        values = levels(rng, shape, shards, -0.22, 0.18) * values
    return jnp.clip(values, min=-bound, max=bound).astype(kind)


def setup_inputs(seed: int = 0) -> dict:
    splits = jax.random.split(jax.random.key(seed), 8)
    return {
        "inputs": normal_values(splits[0], (CLIPS, FRAMES, ROWS, W, C), 1.0, 6.0, ((0, 2), (1, 8), (2, 2)), jnp.float32),
        "weight_one": normal_values(splits[1], (3, 3, 3, C, C), (27 * C) ** -0.5, 0.125, (), jnp.float32),
        "bias_one": normal_values(splits[2], (C,), 1.0, 4.0, (), jnp.float32),
        "gain_one": jnp.clip(1.0 + 0.15 * jax.random.normal(splits[3], (C,), jnp.float32), 0.25, 1.75),
        "weight_two": normal_values(splits[4], (3, 3, 3, C, C), (27 * C) ** -0.5, 0.125, (), jnp.float32),
        "gain_two": jnp.clip(1.0 + 0.15 * jax.random.normal(splits[5], (C,), jnp.float32), 0.25, 1.75),
        "cotangent": normal_values(splits[6], (CLIPS, FRAMES, ROWS, W, C), 1.0, 6.0, ((0, 2), (1, 8), (2, 2)), jnp.float32),
    }


def norm_act(values, scales):
    square = lax.optimization_barrier(jnp.mean(values * values, axis=-1, keepdims=True))
    return jax.nn.silu(values * lax.rsqrt(square + 1e-06) * scales)

def conv_causal(values, kernel):
    return lax.conv_general_dilated(values, kernel, (1, 1, 1), [(2, 0), (1, 1), (1, 1)], dimension_numbers=('NDHWC', 'DHWIO', 'NDHWC'), precision=lax.Precision.HIGHEST)

def block_forward(values, kernel_one, offset_one, scales_one, kernel_two, scales_two):
    acts = norm_act(values, scales_one)
    hidden = conv_causal(acts, kernel_one) + offset_one
    return values + conv_causal(norm_act(hidden, scales_two), kernel_two)

def reference(inputs, weight_one, bias_one, gain_one, weight_two, gain_two, cotangent):
    _, pullback = jax.vjp(block_forward, inputs, weight_one, bias_one, gain_one, weight_two, gain_two)
    grad_in, grad_k1, grad_b1, grad_g1, grad_k2, grad_g2 = pullback(cotangent)
    factor = 1.0 / math.sqrt(CLIPS * FRAMES * ROWS * W)
    second_bias = lax.optimization_barrier(jnp.sum(cotangent, axis=(0, 1, 2, 3)))
    vectors = jnp.stack([grad_b1, second_bias, grad_g1, grad_g2]) * factor
    return (grad_in, grad_k1.reshape(27 * C, C) * factor, grad_k2.reshape(27 * C, C) * factor, vectors)
```

```python
import math

import jax
import jax.numpy as jnp
from jax import lax
from jax.sharding import PartitionSpec as P


def passed_along(block, axis, distance):
    devices = range(lax.axis_size(axis))
    route = [(i - distance, i) for i in devices if i - distance in devices]
    return lax.ppermute(block, axis, route)


def padded(block, sides, width):
    for axis, dim in sides:
        count = lax.axis_size(axis)
        forward = [(i, i + 1) for i in range(count - 1)]
        backward = [(target, source) for source, target in forward]
        low = lax.ppermute(
            lax.slice_in_dim(block, block.shape[dim] - width, None, axis=dim), axis, forward
        )
        high = lax.ppermute(lax.slice_in_dim(block, 0, width, axis=dim), axis, backward)
        block = jnp.concatenate([low, block, high], axis=dim)
    return block


def norm_act(values, scales):
    square = jnp.mean(values * values, axis=-1, keepdims=True)
    return jax.nn.silu(values * lax.rsqrt(square + 1e-06) * scales)


def conv_valid(values, kernel):
    return lax.conv_general_dilated(
        values,
        kernel,
        (1, 1, 1),
        [(0, 0), (0, 0), (1, 1)],
        dimension_numbers=("NDHWC", "DHWIO", "NDHWC"),
        precision=lax.Precision.HIGHEST,
    )


def flipped(kernel):
    return jnp.swapaxes(kernel[::-1, ::-1, ::-1], 3, 4)


def on_device(inputs, weight_one, bias_one, gain_one, weight_two, gain_two, cotangent):
    frames = inputs.shape[1]
    rows = inputs.shape[2]
    acts = norm_act(inputs, gain_one)
    acts_past = passed_along(acts[:, frames - 2 :], "tm", 1)
    acts_wide = padded(jnp.concatenate([acts_past, acts], axis=1), (("height", 2),), 1)
    hidden = conv_valid(acts_wide, weight_one) + bias_one
    gated = norm_act(hidden, gain_two)
    gated_past = passed_along(gated[:, frames - 2 :], "tm", 1)
    gated_wide = padded(jnp.concatenate([gated_past, gated], axis=1), (("height", 2),), 1)
    cot_next = passed_along(cotangent[:, :2], "tm", -1)
    cot_wide = padded(jnp.concatenate([cotangent, cot_next], axis=1), (("height", 2),), 1)
    grad_gated = conv_valid(cot_wide, flipped(weight_two))
    _, pull_two = jax.vjp(lambda kernel: conv_valid(gated_wide, kernel), weight_two)
    (local_two,) = pull_two(cotangent)
    _, pull_norm_two = jax.vjp(norm_act, hidden, gain_two)
    grad_hidden, gain_two_part = pull_norm_two(grad_gated)
    grad_next = passed_along(grad_hidden[:, :2], "tm", -1)
    grad_wide = padded(jnp.concatenate([grad_hidden, grad_next], axis=1), (("height", 2),), 1)
    grad_acts = conv_valid(grad_wide, flipped(weight_one))
    _, pull_one = jax.vjp(lambda kernel: conv_valid(acts_wide, kernel), weight_one)
    (local_one,) = pull_one(grad_hidden)
    _, pull_norm_one = jax.vjp(norm_act, inputs, gain_one)
    grad_part, gain_one_part = pull_norm_one(grad_acts)
    grad_inputs = cotangent + grad_part
    vectors = jnp.stack(
        [
            jnp.sum(grad_hidden, axis=(0, 1, 2, 3)),
            jnp.sum(cotangent, axis=(0, 1, 2, 3)),
            gain_one_part,
            gain_two_part,
        ]
    )
    channels = local_one.shape[4]
    taps = 27 * local_one.shape[3]
    flat_one = local_one.reshape(taps, channels)
    flat_two = local_two.reshape(taps, channels)
    count = (
        inputs.shape[0]
        * frames
        * rows
        * inputs.shape[3]
        * lax.axis_size("tm")
        * lax.axis_size("height")
        * lax.axis_size("batch")
    )
    factor = 1.0 / math.sqrt(count)
    parts = lax.axis_size("tm")
    share = taps // parts
    scaled_two = (flat_two * factor).reshape(parts, share, channels)
    part_two = lax.psum(lax.psum_scatter(scaled_two, "tm", scatter_dimension=0), ("height", "batch"))
    spread = jnp.broadcast_to(vectors * factor, (parts,) + vectors.shape)
    packed = jnp.concatenate([(flat_one * factor).reshape(parts, share, channels), spread], axis=1)
    part_one = lax.psum(lax.psum_scatter(packed, "tm", scatter_dimension=0), ("height", "batch"))
    return (grad_inputs, part_one[:share], part_two, part_one[share:])


def solution(mesh):
    placed = (
        P("batch", "tm", "height", None, None),
        P(),
        P(),
        P(),
        P(),
        P(),
        P("batch", "tm", "height", None, None),
    )
    return jax.shard_map(
        on_device,
        mesh=mesh,
        in_specs=placed,
        out_specs=(P("batch", "tm", "height", None, None), P("tm", None), P("tm", None), P()),
        check_vma=False,
    )
```

```python
import math

import jax
import jax.numpy as jnp
from jax import lax
from jax.sharding import PartitionSpec as P


def passed_along(block, axis, distance):
    devices = range(lax.axis_size(axis))
    route = [(i - distance, i) for i in devices if i - distance in devices]
    return lax.ppermute(block, axis, route)


def padded(block, sides, width):
    for axis, dim in sides:
        count = lax.axis_size(axis)
        forward = [(i, i + 1) for i in range(count - 1)]
        backward = [(target, source) for source, target in forward]
        low = lax.ppermute(
            lax.slice_in_dim(block, block.shape[dim] - width, None, axis=dim), axis, forward
        )
        high = lax.ppermute(lax.slice_in_dim(block, 0, width, axis=dim), axis, backward)
        block = jnp.concatenate([low, block, high], axis=dim)
    return block


def norm_act(values, scales):
    square = jnp.mean(values * values, axis=-1, keepdims=True)
    return jax.nn.silu(values * lax.rsqrt(square + 1e-06) * scales)


def patches(wide):
    frames = wide.shape[1] - 2
    rows = wide.shape[2] - 2
    cols = wide.shape[3]
    edged = jnp.pad(wide, ((0, 0), (0, 0), (0, 0), (1, 1), (0, 0)))
    pieces = [
        edged[:, i : i + frames, j : j + rows, l : l + cols]
        for i in range(3)
        for j in range(3)
        for l in range(3)
    ]
    taps = jnp.concatenate(pieces, axis=-1)
    return taps.reshape(-1, taps.shape[-1])


def conv_taps(taps, kernel, shape):
    out = jnp.dot(taps, kernel.reshape(-1, kernel.shape[-1]), precision=lax.Precision.HIGHEST)
    return out.reshape(shape[:4] + (kernel.shape[-1],))


def kernel_grad(taps, grad):
    flat = grad.reshape(-1, grad.shape[-1])
    return lax.dot_general(taps, flat, (((0,), (0,)), ((), ())), precision=lax.Precision.HIGHEST)


def flipped(kernel):
    return jnp.swapaxes(kernel[::-1, ::-1, ::-1], 3, 4)


def on_device(inputs, weight_one, bias_one, gain_one, weight_two, gain_two, cotangent):
    frames = inputs.shape[1]
    rows = inputs.shape[2]
    acts = norm_act(inputs, gain_one)
    acts_past = passed_along(acts[:, frames - 2 :], "tm", 1)
    acts_wide = padded(jnp.concatenate([acts_past, acts], axis=1), (("height", 2),), 1)
    acts_taps = patches(acts_wide)
    hidden = conv_taps(acts_taps, weight_one, inputs.shape) + bias_one
    gated = norm_act(hidden, gain_two)
    gated_past = passed_along(gated[:, frames - 2 :], "tm", 1)
    gated_wide = padded(jnp.concatenate([gated_past, gated], axis=1), (("height", 2),), 1)
    cot_next = passed_along(cotangent[:, :2], "tm", -1)
    cot_wide = padded(jnp.concatenate([cotangent, cot_next], axis=1), (("height", 2),), 1)
    grad_gated = conv_taps(patches(cot_wide), flipped(weight_two), inputs.shape)
    flat_two = kernel_grad(patches(gated_wide), cotangent)
    _, pull_norm_two = jax.vjp(norm_act, hidden, gain_two)
    grad_hidden, gain_two_part = pull_norm_two(grad_gated)
    grad_next = passed_along(grad_hidden[:, :2], "tm", -1)
    grad_wide = padded(jnp.concatenate([grad_hidden, grad_next], axis=1), (("height", 2),), 1)
    grad_acts = conv_taps(patches(grad_wide), flipped(weight_one), inputs.shape)
    flat_one = kernel_grad(acts_taps, grad_hidden)
    _, pull_norm_one = jax.vjp(norm_act, inputs, gain_one)
    grad_part, gain_one_part = pull_norm_one(grad_acts)
    grad_inputs = cotangent + grad_part
    vectors = jnp.stack(
        [
            jnp.sum(grad_hidden, axis=(0, 1, 2, 3)),
            jnp.sum(cotangent, axis=(0, 1, 2, 3)),
            gain_one_part,
            gain_two_part,
        ]
    )
    channels = flat_one.shape[1]
    taps = flat_one.shape[0]
    count = (
        inputs.shape[0]
        * frames
        * rows
        * inputs.shape[3]
        * lax.axis_size("tm")
        * lax.axis_size("height")
        * lax.axis_size("batch")
    )
    factor = 1.0 / math.sqrt(count)
    parts = lax.axis_size("tm")
    share = taps // parts
    scaled_two = (flat_two * factor).reshape(parts, share, channels)
    part_two = lax.psum(lax.psum_scatter(scaled_two, "tm", scatter_dimension=0), ("height", "batch"))
    spread = jnp.broadcast_to(vectors * factor, (parts,) + vectors.shape)
    packed = jnp.concatenate([(flat_one * factor).reshape(parts, share, channels), spread], axis=1)
    part_one = lax.psum(lax.psum_scatter(packed, "tm", scatter_dimension=0), ("height", "batch"))
    return (grad_inputs, part_one[:share], part_two, part_one[share:])


def solution(mesh):
    placed = (
        P("batch", "tm", "height", None, None),
        P(),
        P(),
        P(),
        P(),
        P(),
        P("batch", "tm", "height", None, None),
    )
    return jax.shard_map(
        on_device,
        mesh=mesh,
        in_specs=placed,
        out_specs=(P("batch", "tm", "height", None, None), P("tm", None), P("tm", None), P()),
        check_vma=False,
    )
```

```python
import math

import jax
import jax.numpy as jnp
from jax import lax
from jax.sharding import PartitionSpec as P


def passed_along(block, axis, distance):
    devices = range(lax.axis_size(axis))
    route = [(i - distance, i) for i in devices if i - distance in devices]
    return lax.ppermute(block, axis, route)


def padded(block, sides, width):
    for axis, dim in sides:
        count = lax.axis_size(axis)
        forward = [(i, i + 1) for i in range(count - 1)]
        backward = [(target, source) for source, target in forward]
        low = lax.ppermute(
            lax.slice_in_dim(block, block.shape[dim] - width, None, axis=dim), axis, forward
        )
        high = lax.ppermute(lax.slice_in_dim(block, 0, width, axis=dim), axis, backward)
        block = jnp.concatenate([low, block, high], axis=dim)
    return block


def norm_act(values, scales):
    square = jnp.mean(values * values, axis=-1, keepdims=True)
    return jax.nn.silu(values * lax.rsqrt(square + 1e-06) * scales)


def patches(wide):
    frames = wide.shape[1] - 2
    rows = wide.shape[2] - 2
    cols = wide.shape[3]
    edged = jnp.pad(wide, ((0, 0), (0, 0), (0, 0), (1, 1), (0, 0)))
    pieces = [
        edged[:, i : i + frames, j : j + rows, l : l + cols]
        for i in range(3)
        for j in range(3)
        for l in range(3)
    ]
    taps = jnp.concatenate(pieces, axis=-1)
    return taps.reshape(-1, taps.shape[-1])


def conv_taps(taps, kernel, shape):
    out = jnp.dot(taps, kernel.reshape(-1, kernel.shape[-1]), precision=lax.Precision.HIGHEST)
    return out.reshape(shape[:4] + (kernel.shape[-1],))


def kernel_grad(taps, grad):
    flat = grad.reshape(-1, grad.shape[-1])
    return lax.dot_general(taps, flat, (((0,), (0,)), ((), ())), precision=lax.Precision.HIGHEST)


def flipped(kernel):
    return jnp.swapaxes(kernel[::-1, ::-1, ::-1], 3, 4)


def exchanged(block, axis, bit):
    count = lax.axis_size(axis)
    return lax.ppermute(block, axis, [(i, i ^ bit) for i in range(count)])


def halved(blocks, axis):
    count = lax.axis_size(axis)
    if count & (count - 1):
        return lax.psum_scatter(blocks, axis, scatter_dimension=0)
    me = lax.axis_index(axis)
    bit = 1
    while bit < count:
        mine = (me // bit) % 2
        pairs = blocks.reshape((blocks.shape[0] // 2, 2) + blocks.shape[1:])
        keep = lax.dynamic_index_in_dim(pairs, mine, axis=1, keepdims=False)
        send = lax.dynamic_index_in_dim(pairs, 1 - mine, axis=1, keepdims=False)
        blocks = keep + exchanged(send, axis, bit)
        bit *= 2
    return blocks[0]


def summed(block, axis):
    count = lax.axis_size(axis)
    if count & (count - 1):
        return lax.psum(block, axis)
    bit = 1
    while bit < count:
        block = block + exchanged(block, axis, bit)
        bit *= 2
    return block


def gathered(block, axis):
    count = lax.axis_size(axis)
    if count & (count - 1):
        return lax.all_gather(block, axis, tiled=True)
    me = lax.axis_index(axis)
    bit = 1
    while bit < count:
        other = exchanged(block, axis, bit)
        low = (me // bit) % 2 == 0
        block = jnp.where(low, jnp.concatenate([block, other]), jnp.concatenate([other, block]))
        bit *= 2
    return block


def reduced(blocks):
    parts, size, channels = blocks.shape
    split = lax.axis_size("height")
    width = -(-size // split)
    blocks = jnp.pad(blocks, ((0, 0), (0, width * split - size), (0, 0)))
    blocks = jnp.swapaxes(blocks.reshape(parts, split, width, channels), 0, 1)
    block = halved(halved(blocks, "height"), "tm")
    return gathered(summed(block, "batch"), "height")[:size]


def on_device(inputs, weight_one, bias_one, gain_one, weight_two, gain_two, cotangent):
    frames = inputs.shape[1]
    rows = inputs.shape[2]
    acts = norm_act(inputs, gain_one)
    acts_past = passed_along(acts[:, frames - 2 :], "tm", 1)
    acts_wide = padded(jnp.concatenate([acts_past, acts], axis=1), (("height", 2),), 1)
    acts_taps = patches(acts_wide)
    hidden = conv_taps(acts_taps, weight_one, inputs.shape) + bias_one
    gated = norm_act(hidden, gain_two)
    gated_past = passed_along(gated[:, frames - 2 :], "tm", 1)
    gated_wide = padded(jnp.concatenate([gated_past, gated], axis=1), (("height", 2),), 1)
    cot_next = passed_along(cotangent[:, :2], "tm", -1)
    cot_wide = padded(jnp.concatenate([cotangent, cot_next], axis=1), (("height", 2),), 1)
    grad_gated = conv_taps(patches(cot_wide), flipped(weight_two), inputs.shape)
    flat_two = kernel_grad(patches(gated_wide), cotangent)
    _, pull_norm_two = jax.vjp(norm_act, hidden, gain_two)
    grad_hidden, gain_two_part = pull_norm_two(grad_gated)
    grad_next = passed_along(grad_hidden[:, :2], "tm", -1)
    grad_wide = padded(jnp.concatenate([grad_hidden, grad_next], axis=1), (("height", 2),), 1)
    grad_acts = conv_taps(patches(grad_wide), flipped(weight_one), inputs.shape)
    flat_one = kernel_grad(acts_taps, grad_hidden)
    _, pull_norm_one = jax.vjp(norm_act, inputs, gain_one)
    grad_part, gain_one_part = pull_norm_one(grad_acts)
    grad_inputs = cotangent + grad_part
    channels = flat_one.shape[1]
    taps = flat_one.shape[0]
    count = (
        inputs.shape[0]
        * frames
        * rows
        * inputs.shape[3]
        * lax.axis_size("tm")
        * lax.axis_size("height")
        * lax.axis_size("batch")
    )
    factor = 1.0 / math.sqrt(count)
    parts = lax.axis_size("tm")
    share = taps // parts
    early = jnp.stack(
        [jnp.sum(grad_hidden, axis=(0, 1, 2, 3)), jnp.sum(cotangent, axis=(0, 1, 2, 3)), gain_two_part]
    )
    packed_two = jnp.concatenate(
        [flat_two.reshape(parts, share, channels), jnp.broadcast_to(early, (parts,) + early.shape)], axis=1
    )
    part_two = reduced(packed_two * factor)
    packed_one = jnp.concatenate(
        [flat_one.reshape(parts, share, channels), jnp.broadcast_to(gain_one_part, (parts, 1, channels))], axis=1
    )
    part_one = reduced(packed_one * factor)
    vectors = jnp.concatenate([part_two[share:], part_one[share:]])[jnp.array([0, 1, 3, 2])]
    return (grad_inputs, part_one[:share], part_two[:share], vectors)


def solution(mesh):
    placed = (
        P("batch", "tm", "height", None, None),
        P(),
        P(),
        P(),
        P(),
        P(),
        P("batch", "tm", "height", None, None),
    )
    return jax.shard_map(
        on_device,
        mesh=mesh,
        in_specs=placed,
        out_specs=(P("batch", "tm", "height", None, None), P("tm", None), P("tm", None), P()),
        check_vma=False,
    )
```

```python
import math

import jax
import jax.numpy as jnp
from jax import lax
from jax.sharding import PartitionSpec as P


def passed_along(block, axis, distance):
    devices = range(lax.axis_size(axis))
    route = [(i - distance, i) for i in devices if i - distance in devices]
    return lax.ppermute(block, axis, route)


def padded(block, sides, width):
    for axis, dim in sides:
        count = lax.axis_size(axis)
        forward = [(i, i + 1) for i in range(count - 1)]
        backward = [(target, source) for source, target in forward]
        low = lax.ppermute(
            lax.slice_in_dim(block, block.shape[dim] - width, None, axis=dim), axis, forward
        )
        high = lax.ppermute(lax.slice_in_dim(block, 0, width, axis=dim), axis, backward)
        block = jnp.concatenate([low, block, high], axis=dim)
    return block


def norm_act(values, scales):
    square = jnp.mean(values * values, axis=-1, keepdims=True)
    return jax.nn.silu(values * lax.rsqrt(square + 1e-06) * scales)


def patches(wide):
    frames = wide.shape[1] - 2
    rows = wide.shape[2] - 2
    cols = wide.shape[3]
    edged = jnp.pad(wide, ((0, 0), (0, 0), (0, 0), (1, 1), (0, 0)))
    pieces = [
        edged[:, i : i + frames, j : j + rows, l : l + cols]
        for i in range(3)
        for j in range(3)
        for l in range(3)
    ]
    taps = jnp.concatenate(pieces, axis=-1)
    return taps.reshape(-1, taps.shape[-1])


def conv_taps(taps, kernel, shape):
    out = jnp.dot(taps, kernel.reshape(-1, kernel.shape[-1]), precision=lax.Precision.HIGHEST)
    return out.reshape(shape[:4] + (kernel.shape[-1],))


def kernel_grad(taps, grad):
    flat = grad.reshape(-1, grad.shape[-1])
    spread = lax.dot_general(flat, taps, (((0,), (0,)), ((), ())), precision=lax.Precision.HIGHEST)
    return spread.T


def flipped(kernel):
    return jnp.swapaxes(kernel[::-1, ::-1, ::-1], 3, 4)


def exchanged(block, axis, bit):
    count = lax.axis_size(axis)
    return lax.ppermute(block, axis, [(i, i ^ bit) for i in range(count)])


def halved(blocks, axis):
    count = lax.axis_size(axis)
    if count & (count - 1):
        return lax.psum_scatter(blocks, axis, scatter_dimension=0)
    me = lax.axis_index(axis)
    bit = 1
    while bit < count:
        mine = (me // bit) % 2
        pairs = blocks.reshape((blocks.shape[0] // 2, 2) + blocks.shape[1:])
        keep = lax.dynamic_index_in_dim(pairs, mine, axis=1, keepdims=False)
        send = lax.dynamic_index_in_dim(pairs, 1 - mine, axis=1, keepdims=False)
        blocks = keep + exchanged(send, axis, bit)
        bit *= 2
    return blocks[0]


def summed(block, axis):
    count = lax.axis_size(axis)
    if count & (count - 1):
        return lax.psum(block, axis)
    bit = 1
    while bit < count:
        block = block + exchanged(block, axis, bit)
        bit *= 2
    return block


def gathered(block, axis):
    count = lax.axis_size(axis)
    if count & (count - 1):
        return lax.all_gather(block, axis, tiled=True)
    me = lax.axis_index(axis)
    bit = 1
    while bit < count:
        other = exchanged(block, axis, bit)
        low = (me // bit) % 2 == 0
        block = jnp.where(low, jnp.concatenate([block, other]), jnp.concatenate([other, block]))
        bit *= 2
    return block


def reduced(blocks):
    parts, size, channels = blocks.shape
    split = lax.axis_size("height")
    width = -(-size // split)
    blocks = jnp.pad(blocks, ((0, 0), (0, width * split - size), (0, 0)))
    blocks = jnp.swapaxes(blocks.reshape(parts, split, width, channels), 0, 1)
    block = halved(halved(blocks, "height"), "tm")
    return gathered(summed(block, "batch"), "height")[:size]


def on_device(inputs, weight_one, bias_one, gain_one, weight_two, gain_two, cotangent):
    frames = inputs.shape[1]
    rows = inputs.shape[2]
    acts = norm_act(inputs, gain_one)
    acts_past = passed_along(acts[:, frames - 2 :], "tm", 1)
    acts_wide = padded(jnp.concatenate([acts_past, acts], axis=1), (("height", 2),), 1)
    acts_taps = patches(acts_wide)
    hidden = conv_taps(acts_taps, weight_one, inputs.shape) + bias_one
    gated = norm_act(hidden, gain_two)
    gated_past = passed_along(gated[:, frames - 2 :], "tm", 1)
    gated_wide = padded(jnp.concatenate([gated_past, gated], axis=1), (("height", 2),), 1)
    cot_next = passed_along(cotangent[:, :2], "tm", -1)
    cot_wide = padded(jnp.concatenate([cotangent, cot_next], axis=1), (("height", 2),), 1)
    grad_gated = conv_taps(patches(cot_wide), flipped(weight_two), inputs.shape)
    flat_two = kernel_grad(patches(gated_wide), cotangent)
    _, pull_norm_two = jax.vjp(norm_act, hidden, gain_two)
    grad_hidden, gain_two_part = pull_norm_two(grad_gated)
    grad_next = passed_along(grad_hidden[:, :2], "tm", -1)
    grad_wide = padded(jnp.concatenate([grad_hidden, grad_next], axis=1), (("height", 2),), 1)
    grad_acts = conv_taps(patches(grad_wide), flipped(weight_one), inputs.shape)
    flat_one = kernel_grad(acts_taps, grad_hidden)
    _, pull_norm_one = jax.vjp(norm_act, inputs, gain_one)
    grad_part, gain_one_part = pull_norm_one(grad_acts)
    grad_inputs = cotangent + grad_part
    channels = flat_one.shape[1]
    taps = flat_one.shape[0]
    count = (
        inputs.shape[0]
        * frames
        * rows
        * inputs.shape[3]
        * lax.axis_size("tm")
        * lax.axis_size("height")
        * lax.axis_size("batch")
    )
    factor = 1.0 / math.sqrt(count)
    parts = lax.axis_size("tm")
    share = taps // parts
    vectors = jnp.stack(
        [
            jnp.sum(grad_hidden, axis=(0, 1, 2, 3)),
            jnp.sum(cotangent, axis=(0, 1, 2, 3)),
            gain_one_part,
            gain_two_part,
        ]
    )
    packed = jnp.concatenate(
        [
            flat_one.reshape(parts, share, channels),
            flat_two.reshape(parts, share, channels),
            jnp.broadcast_to(vectors, (parts,) + vectors.shape),
        ],
        axis=1,
    )
    total = reduced(packed * factor)
    return (grad_inputs, total[:share], total[share : 2 * share], total[2 * share :])


def solution(mesh):
    placed = (
        P("batch", "tm", "height", None, None),
        P(),
        P(),
        P(),
        P(),
        P(),
        P("batch", "tm", "height", None, None),
    )
    return jax.shard_map(
        on_device,
        mesh=mesh,
        in_specs=placed,
        out_specs=(P("batch", "tm", "height", None, None), P("tm", None), P("tm", None), P()),
        check_vma=False,
    )
```

```python
import math

import jax
import jax.numpy as jnp
from jax import lax
from jax.sharding import PartitionSpec as P


def passed_along(block, axis, distance):
    devices = range(lax.axis_size(axis))
    route = [(i - distance, i) for i in devices if i - distance in devices]
    return lax.ppermute(block, axis, route)


def padded(block, sides, width):
    for axis, dim in sides:
        count = lax.axis_size(axis)
        forward = [(i, i + 1) for i in range(count - 1)]
        backward = [(target, source) for source, target in forward]
        low = lax.ppermute(
            lax.slice_in_dim(block, block.shape[dim] - width, None, axis=dim), axis, forward
        )
        high = lax.ppermute(lax.slice_in_dim(block, 0, width, axis=dim), axis, backward)
        block = jnp.concatenate([low, block, high], axis=dim)
    return block


def norm_act(values, scales):
    square = jnp.mean(values * values, axis=-1, keepdims=True)
    return jax.nn.silu(values * lax.rsqrt(square + 1e-06) * scales)


def patches(wide):
    frames = wide.shape[1] - 2
    rows = wide.shape[2] - 2
    cols = wide.shape[3]
    edged = jnp.pad(wide, ((0, 0), (0, 0), (0, 0), (1, 1), (0, 0)))
    pieces = [
        edged[:, i : i + frames, j : j + rows, l : l + cols]
        for i in range(3)
        for j in range(3)
        for l in range(3)
    ]
    taps = jnp.concatenate(pieces, axis=-1)
    return taps.reshape(-1, taps.shape[-1])


def conv_taps(taps, kernel, shape):
    out = jnp.dot(taps, kernel.reshape(-1, kernel.shape[-1]), precision=lax.Precision.HIGH)
    return out.reshape(shape[:4] + (kernel.shape[-1],))


def kernel_grad(taps, grad):
    flat = grad.reshape(-1, grad.shape[-1])
    spread = lax.dot_general(flat, taps, (((0,), (0,)), ((), ())), precision=lax.Precision.HIGH)
    return spread.T


def flipped(kernel):
    return jnp.swapaxes(kernel[::-1, ::-1, ::-1], 3, 4)


def exchanged(block, axis, bit):
    count = lax.axis_size(axis)
    return lax.ppermute(block, axis, [(i, i ^ bit) for i in range(count)])


def halved(blocks, axis):
    count = lax.axis_size(axis)
    if count & (count - 1):
        return lax.psum_scatter(blocks, axis, scatter_dimension=0)
    me = lax.axis_index(axis)
    bit = 1
    while bit < count:
        mine = (me // bit) % 2
        pairs = blocks.reshape((blocks.shape[0] // 2, 2) + blocks.shape[1:])
        keep = lax.dynamic_index_in_dim(pairs, mine, axis=1, keepdims=False)
        send = lax.dynamic_index_in_dim(pairs, 1 - mine, axis=1, keepdims=False)
        blocks = keep + exchanged(send, axis, bit)
        bit *= 2
    return blocks[0]


def summed(block, axis):
    count = lax.axis_size(axis)
    if count & (count - 1):
        return lax.psum(block, axis)
    bit = 1
    while bit < count:
        block = block + exchanged(block, axis, bit)
        bit *= 2
    return block


def gathered(block, axis):
    count = lax.axis_size(axis)
    if count & (count - 1):
        return lax.all_gather(block, axis, tiled=True)
    me = lax.axis_index(axis)
    bit = 1
    while bit < count:
        other = exchanged(block, axis, bit)
        low = (me // bit) % 2 == 0
        block = jnp.where(low, jnp.concatenate([block, other]), jnp.concatenate([other, block]))
        bit *= 2
    return block


def reduced(blocks):
    parts, size, channels = blocks.shape
    split = lax.axis_size("height")
    width = -(-size // split)
    blocks = jnp.pad(blocks, ((0, 0), (0, width * split - size), (0, 0)))
    blocks = jnp.swapaxes(blocks.reshape(parts, split, width, channels), 0, 1)
    block = halved(halved(blocks, "height"), "tm")
    return gathered(summed(block, "batch"), "height")[:size]


def on_device(inputs, weight_one, bias_one, gain_one, weight_two, gain_two, cotangent):
    frames = inputs.shape[1]
    rows = inputs.shape[2]
    acts = norm_act(inputs, gain_one)
    acts_past = passed_along(acts[:, frames - 2 :], "tm", 1)
    acts_wide = padded(jnp.concatenate([acts_past, acts], axis=1), (("height", 2),), 1)
    acts_taps = patches(acts_wide)
    hidden = conv_taps(acts_taps, weight_one, inputs.shape) + bias_one
    gated = norm_act(hidden, gain_two)
    gated_past = passed_along(gated[:, frames - 2 :], "tm", 1)
    gated_wide = padded(jnp.concatenate([gated_past, gated], axis=1), (("height", 2),), 1)
    cot_next = passed_along(cotangent[:, :2], "tm", -1)
    cot_wide = padded(jnp.concatenate([cotangent, cot_next], axis=1), (("height", 2),), 1)
    grad_gated = conv_taps(patches(cot_wide), flipped(weight_two), inputs.shape)
    flat_two = kernel_grad(patches(gated_wide), cotangent)
    _, pull_norm_two = jax.vjp(norm_act, hidden, gain_two)
    grad_hidden, gain_two_part = pull_norm_two(grad_gated)
    grad_next = passed_along(grad_hidden[:, :2], "tm", -1)
    grad_wide = padded(jnp.concatenate([grad_hidden, grad_next], axis=1), (("height", 2),), 1)
    grad_acts = conv_taps(patches(grad_wide), flipped(weight_one), inputs.shape)
    flat_one = kernel_grad(acts_taps, grad_hidden)
    _, pull_norm_one = jax.vjp(norm_act, inputs, gain_one)
    grad_part, gain_one_part = pull_norm_one(grad_acts)
    grad_inputs = cotangent + grad_part
    channels = flat_one.shape[1]
    taps = flat_one.shape[0]
    count = (
        inputs.shape[0]
        * frames
        * rows
        * inputs.shape[3]
        * lax.axis_size("tm")
        * lax.axis_size("height")
        * lax.axis_size("batch")
    )
    factor = 1.0 / math.sqrt(count)
    parts = lax.axis_size("tm")
    share = taps // parts
    vectors = jnp.stack(
        [
            jnp.sum(grad_hidden, axis=(0, 1, 2, 3)),
            jnp.sum(cotangent, axis=(0, 1, 2, 3)),
            gain_one_part,
            gain_two_part,
        ]
    )
    packed = jnp.concatenate(
        [
            flat_one.reshape(parts, share, channels),
            flat_two.reshape(parts, share, channels),
            jnp.broadcast_to(vectors, (parts,) + vectors.shape),
        ],
        axis=1,
    )
    total = reduced(packed * factor)
    return (grad_inputs, total[:share], total[share : 2 * share], total[2 * share :])


def solution(mesh):
    placed = (
        P("batch", "tm", "height", None, None),
        P(),
        P(),
        P(),
        P(),
        P(),
        P("batch", "tm", "height", None, None),
    )
    return jax.shard_map(
        on_device,
        mesh=mesh,
        in_specs=placed,
        out_specs=(P("batch", "tm", "height", None, None), P("tm", None), P("tm", None), P()),
        check_vma=False,
    )
```

```python
import math

import jax
import jax.numpy as jnp
from jax import lax
from jax.sharding import PartitionSpec as P


def passed_along(block, axis, distance):
    devices = range(lax.axis_size(axis))
    route = [(i - distance, i) for i in devices if i - distance in devices]
    return lax.ppermute(block, axis, route)


def padded(block, sides, width):
    for axis, dim in sides:
        count = lax.axis_size(axis)
        forward = [(i, i + 1) for i in range(count - 1)]
        backward = [(target, source) for source, target in forward]
        low = lax.ppermute(
            lax.slice_in_dim(block, block.shape[dim] - width, None, axis=dim), axis, forward
        )
        high = lax.ppermute(lax.slice_in_dim(block, 0, width, axis=dim), axis, backward)
        block = jnp.concatenate([low, block, high], axis=dim)
    return block


def norm_act(values, scales):
    square = jnp.mean(values * values, axis=-1, keepdims=True)
    return jax.nn.silu(values * lax.rsqrt(square + 1e-06) * scales)


def patches(wide):
    frames = wide.shape[1] - 2
    rows = wide.shape[2] - 2
    cols = wide.shape[3]
    edged = jnp.pad(wide, ((0, 0), (0, 0), (0, 0), (1, 1), (0, 0)))
    pieces = [
        edged[:, i : i + frames, j : j + rows, l : l + cols]
        for i in range(3)
        for j in range(3)
        for l in range(3)
    ]
    taps = jnp.concatenate(pieces, axis=-1)
    return taps.reshape(-1, taps.shape[-1])


def conv_taps(taps, kernel, shape):
    out = jnp.dot(taps, kernel.reshape(-1, kernel.shape[-1]), precision=lax.Precision.HIGH)
    return out.reshape(shape[:4] + (kernel.shape[-1],))


def kernel_grad(taps, grad):
    flat = lax.optimization_barrier(grad.reshape(-1, grad.shape[-1]).T)
    spread = lax.optimization_barrier(jnp.dot(flat, taps, precision=lax.Precision.HIGH))
    return spread.T


def flipped(kernel):
    return jnp.swapaxes(kernel[::-1, ::-1, ::-1], 3, 4)


def exchanged(block, axis, bit):
    count = lax.axis_size(axis)
    return lax.ppermute(block, axis, [(i, i ^ bit) for i in range(count)])


def halved(blocks, axis):
    count = lax.axis_size(axis)
    if count & (count - 1):
        return lax.psum_scatter(blocks, axis, scatter_dimension=0)
    me = lax.axis_index(axis)
    bit = 1
    while bit < count:
        mine = (me // bit) % 2
        pairs = blocks.reshape((blocks.shape[0] // 2, 2) + blocks.shape[1:])
        keep = lax.dynamic_index_in_dim(pairs, mine, axis=1, keepdims=False)
        send = lax.dynamic_index_in_dim(pairs, 1 - mine, axis=1, keepdims=False)
        blocks = keep + exchanged(send, axis, bit)
        bit *= 2
    return blocks[0]


def summed(block, axis):
    count = lax.axis_size(axis)
    if count & (count - 1):
        return lax.psum(block, axis)
    bit = 1
    while bit < count:
        block = block + exchanged(block, axis, bit)
        bit *= 2
    return block


def gathered(block, axis):
    count = lax.axis_size(axis)
    if count & (count - 1):
        return lax.all_gather(block, axis, tiled=True)
    me = lax.axis_index(axis)
    bit = 1
    while bit < count:
        other = exchanged(block, axis, bit)
        low = (me // bit) % 2 == 0
        block = jnp.where(low, jnp.concatenate([block, other]), jnp.concatenate([other, block]))
        bit *= 2
    return block


def reduced(blocks):
    parts, size, channels = blocks.shape
    split = lax.axis_size("height")
    width = -(-size // split)
    blocks = jnp.pad(blocks, ((0, 0), (0, width * split - size), (0, 0)))
    blocks = jnp.swapaxes(blocks.reshape(parts, split, width, channels), 0, 1)
    block = halved(halved(blocks, "height"), "tm")
    return gathered(summed(block, "batch"), "height")[:size]


def on_device(inputs, weight_one, bias_one, gain_one, weight_two, gain_two, cotangent):
    frames = inputs.shape[1]
    rows = inputs.shape[2]
    acts = norm_act(inputs, gain_one)
    acts_past = passed_along(acts[:, frames - 2 :], "tm", 1)
    acts_wide = padded(jnp.concatenate([acts_past, acts], axis=1), (("height", 2),), 1)
    acts_taps = patches(acts_wide)
    hidden = conv_taps(acts_taps, weight_one, inputs.shape) + bias_one
    gated = norm_act(hidden, gain_two)
    gated_past = passed_along(gated[:, frames - 2 :], "tm", 1)
    gated_wide = padded(jnp.concatenate([gated_past, gated], axis=1), (("height", 2),), 1)
    cot_next = passed_along(cotangent[:, :2], "tm", -1)
    cot_wide = padded(jnp.concatenate([cotangent, cot_next], axis=1), (("height", 2),), 1)
    grad_gated = conv_taps(patches(cot_wide), flipped(weight_two), inputs.shape)
    flat_two = kernel_grad(patches(gated_wide), cotangent)
    _, pull_norm_two = jax.vjp(norm_act, hidden, gain_two)
    grad_hidden, gain_two_part = pull_norm_two(grad_gated)
    grad_next = passed_along(grad_hidden[:, :2], "tm", -1)
    grad_wide = padded(jnp.concatenate([grad_hidden, grad_next], axis=1), (("height", 2),), 1)
    grad_acts = conv_taps(patches(grad_wide), flipped(weight_one), inputs.shape)
    flat_one = kernel_grad(acts_taps, grad_hidden)
    _, pull_norm_one = jax.vjp(norm_act, inputs, gain_one)
    grad_part, gain_one_part = pull_norm_one(grad_acts)
    grad_inputs = cotangent + grad_part
    channels = flat_one.shape[1]
    taps = flat_one.shape[0]
    count = (
        inputs.shape[0]
        * frames
        * rows
        * inputs.shape[3]
        * lax.axis_size("tm")
        * lax.axis_size("height")
        * lax.axis_size("batch")
    )
    factor = 1.0 / math.sqrt(count)
    parts = lax.axis_size("tm")
    share = taps // parts
    vectors = jnp.stack(
        [
            jnp.sum(grad_hidden, axis=(0, 1, 2, 3)),
            jnp.sum(cotangent, axis=(0, 1, 2, 3)),
            gain_one_part,
            gain_two_part,
        ]
    )
    packed = jnp.concatenate(
        [
            flat_one.reshape(parts, share, channels),
            flat_two.reshape(parts, share, channels),
            jnp.broadcast_to(vectors, (parts,) + vectors.shape),
        ],
        axis=1,
    )
    total = reduced(packed * factor)
    return (grad_inputs, total[:share], total[share : 2 * share], total[2 * share :])


def solution(mesh):
    placed = (
        P("batch", "tm", "height", None, None),
        P(),
        P(),
        P(),
        P(),
        P(),
        P("batch", "tm", "height", None, None),
    )
    return jax.shard_map(
        on_device,
        mesh=mesh,
        in_specs=placed,
        out_specs=(P("batch", "tm", "height", None, None), P("tm", None), P("tm", None), P()),
        check_vma=False,
    )
```

```python
import math

import jax
import jax.numpy as jnp
from jax import lax
from jax.sharding import PartitionSpec as P


def passed_along(block, axis, distance):
    devices = range(lax.axis_size(axis))
    route = [(i - distance, i) for i in devices if i - distance in devices]
    return lax.ppermute(block, axis, route)


def padded(block, sides, width):
    for axis, dim in sides:
        count = lax.axis_size(axis)
        forward = [(i, i + 1) for i in range(count - 1)]
        backward = [(target, source) for source, target in forward]
        low = lax.ppermute(
            lax.slice_in_dim(block, block.shape[dim] - width, None, axis=dim), axis, forward
        )
        high = lax.ppermute(lax.slice_in_dim(block, 0, width, axis=dim), axis, backward)
        block = jnp.concatenate([low, block, high], axis=dim)
    return block


def norm_act(values, scales):
    square = jnp.mean(values * values, axis=-1, keepdims=True)
    return jax.nn.silu(values * lax.rsqrt(square + 1e-06) * scales)


def patches(wide):
    frames = wide.shape[1] - 2
    rows = wide.shape[2] - 2
    cols = wide.shape[3]
    edged = jnp.pad(wide, ((0, 0), (0, 0), (0, 0), (1, 1), (0, 0)))
    pieces = [
        edged[:, i : i + frames, j : j + rows, l : l + cols]
        for i in range(3)
        for j in range(3)
        for l in range(3)
    ]
    taps = jnp.concatenate(pieces, axis=-1)
    return taps.reshape(-1, taps.shape[-1])


def conv_taps(taps, kernel, shape):
    out = jnp.dot(taps, kernel.reshape(-1, kernel.shape[-1]), precision=lax.Precision.HIGH)
    return out.reshape(shape[:4] + (kernel.shape[-1],))


def kernel_grad(taps, grad):
    flat = lax.optimization_barrier(grad.reshape(-1, grad.shape[-1]).T)
    spread = lax.optimization_barrier(jnp.dot(flat, taps, precision=lax.Precision.HIGH))
    return spread.T


def flipped(kernel):
    return jnp.swapaxes(kernel[::-1, ::-1, ::-1], 3, 4)


def exchanged(block, axis, bit):
    count = lax.axis_size(axis)
    return lax.ppermute(block, axis, [(i, i ^ bit) for i in range(count)])


def halved(blocks, axis):
    count = lax.axis_size(axis)
    if count & (count - 1):
        return lax.psum_scatter(blocks, axis, scatter_dimension=0)
    me = lax.axis_index(axis)
    bit = 1
    while bit < count:
        mine = (me // bit) % 2
        pairs = blocks.reshape((blocks.shape[0] // 2, 2) + blocks.shape[1:])
        keep = lax.dynamic_index_in_dim(pairs, mine, axis=1, keepdims=False)
        send = lax.dynamic_index_in_dim(pairs, 1 - mine, axis=1, keepdims=False)
        blocks = keep + exchanged(send, axis, bit)
        blocks = yield blocks
        bit *= 2
    return blocks[0]


def summed(block, axis):
    count = lax.axis_size(axis)
    if count & (count - 1):
        return lax.psum(block, axis)
    bit = 1
    while bit < count:
        block = block + exchanged(block, axis, bit)
        block = yield block
        bit *= 2
    return block


def gathered(block, axis):
    count = lax.axis_size(axis)
    if count & (count - 1):
        return lax.all_gather(block, axis, tiled=True)
    me = lax.axis_index(axis)
    bit = 1
    while bit < count:
        other = exchanged(block, axis, bit)
        low = (me // bit) % 2 == 0
        block = jnp.where(low, jnp.concatenate([block, other]), jnp.concatenate([other, block]))
        block = yield block
        bit *= 2
    return block


def reducing(blocks):
    parts, size, channels = blocks.shape
    split = lax.axis_size("height")
    width = -(-size // split)
    blocks = jnp.pad(blocks, ((0, 0), (0, width * split - size), (0, 0)))
    blocks = jnp.swapaxes(blocks.reshape(parts, split, width, channels), 0, 1)
    block = yield from halved(blocks, "height")
    block = yield from halved(block, "tm")
    block = yield from summed(block, "batch")
    block = yield from gathered(block, "height")
    return block[:size]


def total_sum(block):
    block = yield from summed(block, "tm")
    block = yield from summed(block, "height")
    block = yield from summed(block, "batch")
    return block


def stepped(chain, state):
    try:
        return chain.send(state), False
    except StopIteration as stop:
        return stop.value, True


def finished(chain):
    state, done = stepped(chain, None)
    while not done:
        state, done = stepped(chain, state)
    return state


def on_device(inputs, weight_one, bias_one, gain_one, weight_two, gain_two, cotangent):
    frames = inputs.shape[1]
    rows = inputs.shape[2]
    acts = norm_act(inputs, gain_one)
    acts_past = passed_along(acts[:, frames - 2 :], "tm", 1)
    acts_wide = padded(jnp.concatenate([acts_past, acts], axis=1), (("height", 2),), 1)
    acts_taps = patches(acts_wide)
    hidden = conv_taps(acts_taps, weight_one, inputs.shape) + bias_one
    gated = norm_act(hidden, gain_two)
    gated_past = passed_along(gated[:, frames - 2 :], "tm", 1)
    gated_wide = padded(jnp.concatenate([gated_past, gated], axis=1), (("height", 2),), 1)
    cot_next = passed_along(cotangent[:, :2], "tm", -1)
    cot_wide = padded(jnp.concatenate([cotangent, cot_next], axis=1), (("height", 2),), 1)
    grad_gated = conv_taps(patches(cot_wide), flipped(weight_two), inputs.shape)
    flat_two = kernel_grad(patches(gated_wide), cotangent)
    _, pull_norm_two = jax.vjp(norm_act, hidden, gain_two)
    grad_hidden, gain_two_part = pull_norm_two(grad_gated)
    grad_next = passed_along(grad_hidden[:, :2], "tm", -1)
    grad_wide = padded(jnp.concatenate([grad_hidden, grad_next], axis=1), (("height", 2),), 1)
    flat_one = kernel_grad(acts_taps, grad_hidden)
    channels = flat_one.shape[1]
    taps = flat_one.shape[0]
    count = (
        inputs.shape[0]
        * frames
        * rows
        * inputs.shape[3]
        * lax.axis_size("tm")
        * lax.axis_size("height")
        * lax.axis_size("batch")
    )
    factor = 1.0 / math.sqrt(count)
    parts = lax.axis_size("tm")
    share = taps // parts
    early = jnp.stack(
        [jnp.sum(grad_hidden, axis=(0, 1, 2, 3)), jnp.sum(cotangent, axis=(0, 1, 2, 3)), gain_two_part]
    )
    packed = jnp.concatenate(
        [
            flat_one.reshape(parts, share, channels),
            flat_two.reshape(parts, share, channels),
            jnp.broadcast_to(early, (parts,) + early.shape),
        ],
        axis=1,
    )
    chain = reducing(packed * factor)
    state, done = stepped(chain, None)
    grad_taps = patches(grad_wide)
    state, grad_taps = lax.optimization_barrier((state, grad_taps))
    if not done:
        state, done = stepped(chain, state)
    grad_acts = conv_taps(grad_taps, flipped(weight_one), inputs.shape)
    state, grad_acts = lax.optimization_barrier((state, grad_acts))
    if not done:
        state, done = stepped(chain, state)
    _, pull_norm_one = jax.vjp(norm_act, inputs, gain_one)
    grad_part, gain_one_part = pull_norm_one(grad_acts)
    grad_inputs = cotangent + grad_part
    state, grad_inputs = lax.optimization_barrier((state, grad_inputs))
    while not done:
        state, done = stepped(chain, state)
    gain_one_total = finished(total_sum(gain_one_part[None] * factor))
    vectors = jnp.concatenate([state[2 * share : 2 * share + 2], gain_one_total, state[2 * share + 2 :]])
    return (grad_inputs, state[:share], state[share : 2 * share], vectors)


def solution(mesh):
    placed = (
        P("batch", "tm", "height", None, None),
        P(),
        P(),
        P(),
        P(),
        P(),
        P("batch", "tm", "height", None, None),
    )
    return jax.shard_map(
        on_device,
        mesh=mesh,
        in_specs=placed,
        out_specs=(P("batch", "tm", "height", None, None), P("tm", None), P("tm", None), P()),
        check_vma=False,
    )
```

```python
import math

import jax
import jax.numpy as jnp
from jax import lax
from jax.sharding import PartitionSpec as P


def passed_along(block, axis, distance):
    devices = range(lax.axis_size(axis))
    route = [(i - distance, i) for i in devices if i - distance in devices]
    return lax.ppermute(block, axis, route)


def padded(block, sides, width):
    for axis, dim in sides:
        count = lax.axis_size(axis)
        forward = [(i, i + 1) for i in range(count - 1)]
        backward = [(target, source) for source, target in forward]
        low = lax.ppermute(
            lax.slice_in_dim(block, block.shape[dim] - width, None, axis=dim), axis, forward
        )
        high = lax.ppermute(lax.slice_in_dim(block, 0, width, axis=dim), axis, backward)
        block = jnp.concatenate([low, block, high], axis=dim)
    return block


def norm_act(values, scales):
    square = jnp.mean(values * values, axis=-1, keepdims=True)
    return jax.nn.silu(values * lax.rsqrt(square + 1e-06) * scales)


def patches(wide):
    frames = wide.shape[1] - 2
    rows = wide.shape[2] - 2
    cols = wide.shape[3]
    edged = jnp.pad(wide, ((0, 0), (0, 0), (0, 0), (1, 1), (0, 0)))
    pieces = [
        edged[:, i : i + frames, j : j + rows, l : l + cols]
        for i in range(3)
        for j in range(3)
        for l in range(3)
    ]
    taps = jnp.concatenate(pieces, axis=-1)
    return taps.reshape(-1, taps.shape[-1])


def conv_taps(taps, kernel, shape):
    out = jnp.dot(taps, kernel.reshape(-1, kernel.shape[-1]), precision=lax.Precision.HIGH)
    return out.reshape(shape[:4] + (kernel.shape[-1],))


def kernel_grad(taps, grad):
    flat = lax.optimization_barrier(grad.reshape(-1, grad.shape[-1]).T)
    spread = lax.optimization_barrier(jnp.dot(flat, taps, precision=lax.Precision.HIGH))
    return spread.T


def kernel_grad_flipped(values, taps):
    channels = values.shape[-1]
    flat = lax.optimization_barrier(values.reshape(-1, channels).T)
    spread = lax.optimization_barrier(jnp.dot(flat, taps, precision=lax.Precision.HIGH))
    spread = spread.reshape(channels, 27, -1)[:, ::-1]
    return jnp.swapaxes(spread, 0, 1).reshape(27 * channels, -1)


def flipped(kernel):
    return jnp.swapaxes(kernel[::-1, ::-1, ::-1], 3, 4)


def exchanged(block, axis, bit):
    count = lax.axis_size(axis)
    return lax.ppermute(block, axis, [(i, i ^ bit) for i in range(count)])


def halved(blocks, axis):
    count = lax.axis_size(axis)
    if count & (count - 1):
        return lax.psum_scatter(blocks, axis, scatter_dimension=0)
    me = lax.axis_index(axis)
    bit = 1
    while bit < count:
        mine = (me // bit) % 2
        pairs = blocks.reshape((blocks.shape[0] // 2, 2) + blocks.shape[1:])
        keep = lax.dynamic_index_in_dim(pairs, mine, axis=1, keepdims=False)
        send = lax.dynamic_index_in_dim(pairs, 1 - mine, axis=1, keepdims=False)
        blocks = keep + exchanged(send, axis, bit)
        bit *= 2
    return blocks[0]


def summed(block, axis):
    count = lax.axis_size(axis)
    if count & (count - 1):
        return lax.psum(block, axis)
    bit = 1
    while bit < count:
        block = block + exchanged(block, axis, bit)
        bit *= 2
    return block


def gathered(block, axis):
    count = lax.axis_size(axis)
    if count & (count - 1):
        return lax.all_gather(block, axis, tiled=True)
    me = lax.axis_index(axis)
    bit = 1
    while bit < count:
        other = exchanged(block, axis, bit)
        low = (me // bit) % 2 == 0
        block = jnp.where(low, jnp.concatenate([block, other]), jnp.concatenate([other, block]))
        bit *= 2
    return block


def reduced(blocks):
    parts, size, channels = blocks.shape
    split = lax.axis_size("height")
    width = -(-size // split)
    blocks = jnp.pad(blocks, ((0, 0), (0, width * split - size), (0, 0)))
    blocks = jnp.swapaxes(blocks.reshape(parts, split, width, channels), 0, 1)
    block = halved(halved(blocks, "height"), "tm")
    return gathered(summed(block, "batch"), "height")[:size]


def on_device(inputs, weight_one, bias_one, gain_one, weight_two, gain_two, cotangent):
    frames = inputs.shape[1]
    rows = inputs.shape[2]
    acts = norm_act(inputs, gain_one)
    acts_past = passed_along(acts[:, frames - 2 :], "tm", 1)
    acts_wide = padded(jnp.concatenate([acts_past, acts], axis=1), (("height", 2),), 1)
    acts_taps = patches(acts_wide)
    hidden = conv_taps(acts_taps, weight_one, inputs.shape) + bias_one
    gated = norm_act(hidden, gain_two)
    cot_next = passed_along(cotangent[:, :2], "tm", -1)
    cot_wide = padded(jnp.concatenate([cotangent, cot_next], axis=1), (("height", 2),), 1)
    cot_taps = patches(cot_wide)
    grad_gated = conv_taps(cot_taps, flipped(weight_two), inputs.shape)
    flat_two = kernel_grad_flipped(gated, cot_taps)
    _, pull_norm_two = jax.vjp(norm_act, hidden, gain_two)
    grad_hidden, gain_two_part = pull_norm_two(grad_gated)
    grad_next = passed_along(grad_hidden[:, :2], "tm", -1)
    grad_wide = padded(jnp.concatenate([grad_hidden, grad_next], axis=1), (("height", 2),), 1)
    grad_acts = conv_taps(patches(grad_wide), flipped(weight_one), inputs.shape)
    flat_one = kernel_grad(acts_taps, grad_hidden)
    _, pull_norm_one = jax.vjp(norm_act, inputs, gain_one)
    grad_part, gain_one_part = pull_norm_one(grad_acts)
    grad_inputs = cotangent + grad_part
    channels = flat_one.shape[1]
    taps = flat_one.shape[0]
    count = (
        inputs.shape[0]
        * frames
        * rows
        * inputs.shape[3]
        * lax.axis_size("tm")
        * lax.axis_size("height")
        * lax.axis_size("batch")
    )
    factor = 1.0 / math.sqrt(count)
    parts = lax.axis_size("tm")
    share = taps // parts
    vectors = jnp.stack(
        [
            jnp.sum(grad_hidden, axis=(0, 1, 2, 3)),
            jnp.sum(cotangent, axis=(0, 1, 2, 3)),
            gain_one_part,
            gain_two_part,
        ]
    )
    packed = jnp.concatenate(
        [
            flat_one.reshape(parts, share, channels),
            flat_two.reshape(parts, share, channels),
            jnp.broadcast_to(vectors, (parts,) + vectors.shape),
        ],
        axis=1,
    )
    total = reduced(packed * factor)
    return (grad_inputs, total[:share], total[share : 2 * share], total[2 * share :])


def solution(mesh):
    placed = (
        P("batch", "tm", "height", None, None),
        P(),
        P(),
        P(),
        P(),
        P(),
        P("batch", "tm", "height", None, None),
    )
    return jax.shard_map(
        on_device,
        mesh=mesh,
        in_specs=placed,
        out_specs=(P("batch", "tm", "height", None, None), P("tm", None), P("tm", None), P()),
        check_vma=False,
    )
```

```python
import math

import jax
import jax.numpy as jnp
from jax import lax
from jax.sharding import PartitionSpec as P


def passed_along(block, axis, distance):
    devices = range(lax.axis_size(axis))
    route = [(i - distance, i) for i in devices if i - distance in devices]
    return lax.ppermute(block, axis, route)


def padded(block, sides, width):
    for axis, dim in sides:
        count = lax.axis_size(axis)
        top = lax.slice_in_dim(block, block.shape[dim] - width, None, axis=dim)
        bottom = lax.slice_in_dim(block, 0, width, axis=dim)
        if count == 2:
            first = lax.axis_index(axis) == 0
            got = lax.ppermute(jnp.where(first, top, bottom), axis, [(0, 1), (1, 0)])
            empty = jnp.zeros_like(got)
            low = jnp.where(first, empty, got)
            high = jnp.where(first, got, empty)
        else:
            forward = [(i, i + 1) for i in range(count - 1)]
            backward = [(target, source) for source, target in forward]
            low = lax.ppermute(top, axis, forward)
            high = lax.ppermute(bottom, axis, backward)
        block = jnp.concatenate([low, block, high], axis=dim)
    return block


def norm_act(values, scales):
    square = jnp.mean(values * values, axis=-1, keepdims=True)
    return jax.nn.silu(values * lax.rsqrt(square + 1e-06) * scales)


def patches(wide):
    frames = wide.shape[1] - 2
    rows = wide.shape[2] - 2
    cols = wide.shape[3]
    edged = jnp.pad(wide, ((0, 0), (0, 0), (0, 0), (1, 1), (0, 0)))
    pieces = [
        edged[:, i : i + frames, j : j + rows, l : l + cols]
        for i in range(3)
        for j in range(3)
        for l in range(3)
    ]
    taps = jnp.concatenate(pieces, axis=-1)
    return taps.reshape(-1, taps.shape[-1])


def conv_taps(taps, kernel, shape):
    out = jnp.dot(taps, kernel.reshape(-1, kernel.shape[-1]), precision=lax.Precision.HIGH)
    return out.reshape(shape[:4] + (kernel.shape[-1],))


def kernel_grad(taps, grad):
    flat = lax.optimization_barrier(grad.reshape(-1, grad.shape[-1]).T)
    spread = lax.optimization_barrier(jnp.dot(flat, taps, precision=lax.Precision.HIGH))
    return spread.T


def kernel_grad_flipped(values, taps):
    channels = values.shape[-1]
    flat = lax.optimization_barrier(values.reshape(-1, channels).T)
    spread = lax.optimization_barrier(jnp.dot(flat, taps, precision=lax.Precision.HIGH))
    spread = spread.reshape(channels, 27, -1)[:, ::-1]
    return jnp.swapaxes(spread, 0, 1).reshape(27 * channels, -1)


def flipped(kernel):
    return jnp.swapaxes(kernel[::-1, ::-1, ::-1], 3, 4)


def exchanged(block, axis, bit):
    count = lax.axis_size(axis)
    return lax.ppermute(block, axis, [(i, i ^ bit) for i in range(count)])


def halved(blocks, axis):
    count = lax.axis_size(axis)
    if count & (count - 1):
        return lax.psum_scatter(blocks, axis, scatter_dimension=0)
    me = lax.axis_index(axis)
    bit = 1
    while bit < count:
        mine = (me // bit) % 2
        pairs = blocks.reshape((blocks.shape[0] // 2, 2) + blocks.shape[1:])
        keep = lax.dynamic_index_in_dim(pairs, mine, axis=1, keepdims=False)
        send = lax.dynamic_index_in_dim(pairs, 1 - mine, axis=1, keepdims=False)
        blocks = keep + exchanged(send, axis, bit)
        bit *= 2
    return blocks[0]


def summed(block, axis):
    count = lax.axis_size(axis)
    if count & (count - 1):
        return lax.psum(block, axis)
    bit = 1
    while bit < count:
        block = block + exchanged(block, axis, bit)
        bit *= 2
    return block


def gathered(block, axis):
    count = lax.axis_size(axis)
    if count & (count - 1):
        return lax.all_gather(block, axis, tiled=True)
    me = lax.axis_index(axis)
    bit = 1
    while bit < count:
        other = exchanged(block, axis, bit)
        low = (me // bit) % 2 == 0
        block = jnp.where(low, jnp.concatenate([block, other]), jnp.concatenate([other, block]))
        bit *= 2
    return block


def reduced(blocks):
    parts, size, channels = blocks.shape
    split = lax.axis_size("height")
    width = -(-size // split)
    blocks = jnp.pad(blocks, ((0, 0), (0, width * split - size), (0, 0)))
    blocks = jnp.swapaxes(blocks.reshape(parts, split, width, channels), 0, 1)
    block = halved(halved(blocks, "height"), "tm")
    return gathered(summed(block, "batch"), "height")[:size]


def on_device(inputs, weight_one, bias_one, gain_one, weight_two, gain_two, cotangent):
    frames = inputs.shape[1]
    rows = inputs.shape[2]
    acts = norm_act(inputs, gain_one)
    acts_past = passed_along(acts[:, frames - 2 :], "tm", 1)
    cot_next = passed_along(cotangent[:, :2], "tm", -1)
    both = jnp.concatenate(
        [jnp.concatenate([acts_past, acts], axis=1), jnp.concatenate([cotangent, cot_next], axis=1)]
    )
    both = padded(both, (("height", 2),), 1)
    acts_wide = both[: inputs.shape[0]]
    cot_wide = both[inputs.shape[0] :]
    acts_taps = patches(acts_wide)
    hidden = conv_taps(acts_taps, weight_one, inputs.shape) + bias_one
    gated = norm_act(hidden, gain_two)
    cot_taps = patches(cot_wide)
    grad_gated = conv_taps(cot_taps, flipped(weight_two), inputs.shape)
    flat_two = kernel_grad_flipped(gated, cot_taps)
    _, pull_norm_two = jax.vjp(norm_act, hidden, gain_two)
    grad_hidden, gain_two_part = pull_norm_two(grad_gated)
    grad_next = passed_along(grad_hidden[:, :2], "tm", -1)
    grad_wide = padded(jnp.concatenate([grad_hidden, grad_next], axis=1), (("height", 2),), 1)
    grad_acts = conv_taps(patches(grad_wide), flipped(weight_one), inputs.shape)
    flat_one = kernel_grad(acts_taps, grad_hidden)
    _, pull_norm_one = jax.vjp(norm_act, inputs, gain_one)
    grad_part, gain_one_part = pull_norm_one(grad_acts)
    grad_inputs = cotangent + grad_part
    channels = flat_one.shape[1]
    taps = flat_one.shape[0]
    count = (
        inputs.shape[0]
        * frames
        * rows
        * inputs.shape[3]
        * lax.axis_size("tm")
        * lax.axis_size("height")
        * lax.axis_size("batch")
    )
    factor = 1.0 / math.sqrt(count)
    parts = lax.axis_size("tm")
    share = taps // parts
    vectors = jnp.stack(
        [
            jnp.sum(grad_hidden, axis=(0, 1, 2, 3)),
            jnp.sum(cotangent, axis=(0, 1, 2, 3)),
            gain_one_part,
            gain_two_part,
        ]
    )
    packed = jnp.concatenate(
        [
            flat_one.reshape(parts, share, channels),
            flat_two.reshape(parts, share, channels),
            jnp.broadcast_to(vectors, (parts,) + vectors.shape),
        ],
        axis=1,
    )
    total = reduced(packed * factor)
    return (grad_inputs, total[:share], total[share : 2 * share], total[2 * share :])


def solution(mesh):
    placed = (
        P("batch", "tm", "height", None, None),
        P(),
        P(),
        P(),
        P(),
        P(),
        P("batch", "tm", "height", None, None),
    )
    return jax.shard_map(
        on_device,
        mesh=mesh,
        in_specs=placed,
        out_specs=(P("batch", "tm", "height", None, None), P("tm", None), P("tm", None), P()),
        check_vma=False,
    )
```

```python
import math

import jax
import jax.numpy as jnp
from jax import lax
from jax.sharding import PartitionSpec as P


def passed_along(block, axis, distance):
    devices = range(lax.axis_size(axis))
    route = [(i - distance, i) for i in devices if i - distance in devices]
    return lax.ppermute(block, axis, route)


def padded(block, sides, width):
    for axis, dim in sides:
        count = lax.axis_size(axis)
        top = lax.slice_in_dim(block, block.shape[dim] - width, None, axis=dim)
        bottom = lax.slice_in_dim(block, 0, width, axis=dim)
        if count == 2:
            first = lax.axis_index(axis) == 0
            got = lax.ppermute(jnp.where(first, top, bottom), axis, [(0, 1), (1, 0)])
            empty = jnp.zeros_like(got)
            low = jnp.where(first, empty, got)
            high = jnp.where(first, got, empty)
        else:
            forward = [(i, i + 1) for i in range(count - 1)]
            backward = [(target, source) for source, target in forward]
            low = lax.ppermute(top, axis, forward)
            high = lax.ppermute(bottom, axis, backward)
        block = jnp.concatenate([low, block, high], axis=dim)
    return block


def norm_act(values, scales):
    square = jnp.mean(values * values, axis=-1, keepdims=True)
    return jax.nn.silu(values * lax.rsqrt(square + 1e-06) * scales)


def patches(wide):
    frames = wide.shape[1] - 2
    rows = wide.shape[2] - 2
    cols = wide.shape[3]
    edged = jnp.pad(wide, ((0, 0), (0, 0), (0, 0), (1, 1), (0, 0)))
    pieces = [
        edged[:, i : i + frames, j : j + rows, l : l + cols]
        for i in range(3)
        for j in range(3)
        for l in range(3)
    ]
    taps = jnp.concatenate(pieces, axis=-1)
    return taps.reshape(-1, taps.shape[-1])


def conv_taps(taps, kernel, shape):
    out = jnp.dot(taps, kernel.reshape(-1, kernel.shape[-1]), precision=lax.Precision.HIGH)
    return out.reshape(shape[:4] + (kernel.shape[-1],))


def kernel_grad(taps, grad):
    flat = lax.optimization_barrier(grad.reshape(-1, grad.shape[-1]).T)
    spread = lax.optimization_barrier(jnp.dot(flat, taps, precision=lax.Precision.HIGH))
    return spread.T


def kernel_grad_flipped(values, taps):
    channels = values.shape[-1]
    flat = lax.optimization_barrier(values.reshape(-1, channels).T)
    spread = lax.optimization_barrier(jnp.dot(flat, taps, precision=lax.Precision.HIGH))
    spread = spread.reshape(channels, 27, -1)[:, ::-1]
    return jnp.swapaxes(spread, 0, 1).reshape(27 * channels, -1)


def flipped(kernel):
    return jnp.swapaxes(kernel[::-1, ::-1, ::-1], 3, 4)


def exchanged(block, axis, bit):
    count = lax.axis_size(axis)
    return lax.ppermute(block, axis, [(i, i ^ bit) for i in range(count)])


def halved(blocks, axis):
    count = lax.axis_size(axis)
    if count & (count - 1):
        return lax.psum_scatter(blocks, axis, scatter_dimension=0)
    me = lax.axis_index(axis)
    bit = 1
    while bit < count:
        mine = (me // bit) % 2
        pairs = blocks.reshape((blocks.shape[0] // 2, 2) + blocks.shape[1:])
        keep = lax.dynamic_index_in_dim(pairs, mine, axis=1, keepdims=False)
        send = lax.dynamic_index_in_dim(pairs, 1 - mine, axis=1, keepdims=False)
        blocks = keep + exchanged(send, axis, bit)
        bit *= 2
    return blocks[0]


def summed(block, axis):
    count = lax.axis_size(axis)
    if count & (count - 1):
        return lax.psum(block, axis)
    bit = 1
    while bit < count:
        block = block + exchanged(block, axis, bit)
        bit *= 2
    return block


def gathered(block, axis):
    count = lax.axis_size(axis)
    if count & (count - 1):
        return lax.all_gather(block, axis, tiled=True)
    me = lax.axis_index(axis)
    bit = 1
    while bit < count:
        other = exchanged(block, axis, bit)
        low = (me // bit) % 2 == 0
        block = jnp.where(low, jnp.concatenate([block, other]), jnp.concatenate([other, block]))
        bit *= 2
    return block


def reduced(blocks):
    parts, size, channels = blocks.shape
    split = lax.axis_size("height")
    width = -(-size // split)
    blocks = jnp.pad(blocks, ((0, 0), (0, width * split - size), (0, 0)))
    blocks = jnp.swapaxes(blocks.reshape(parts, split, width, channels), 0, 1)
    block = halved(halved(blocks, "height"), "tm")
    return gathered(summed(block, "batch"), "height")[:size]


def on_device(inputs, weight_one, bias_one, gain_one, weight_two, gain_two, cotangent):
    frames = inputs.shape[1]
    rows = inputs.shape[2]
    acts = norm_act(inputs, gain_one)
    acts_past = passed_along(acts[:, frames - 2 :], "tm", 1)
    cot_next = passed_along(cotangent[:, :2], "tm", -1)
    both = jnp.concatenate(
        [jnp.concatenate([acts_past, acts], axis=1), jnp.concatenate([cotangent, cot_next], axis=1)]
    )
    both = padded(both, (("height", 2),), 1)
    acts_wide = both[: inputs.shape[0]]
    cot_wide = both[inputs.shape[0] :]
    acts_taps = patches(acts_wide)
    hidden = conv_taps(acts_taps, weight_one, inputs.shape) + bias_one
    gated = norm_act(hidden, gain_two)
    cot_taps = patches(cot_wide)
    grad_gated = conv_taps(cot_taps, flipped(weight_two), inputs.shape)
    flat_two = kernel_grad_flipped(gated, cot_taps)
    _, pull_norm_two = jax.vjp(norm_act, hidden, gain_two)
    grad_hidden, gain_two_part = pull_norm_two(grad_gated)
    grad_next = passed_along(grad_hidden[:, :2], "tm", -1)
    grad_wide = padded(jnp.concatenate([grad_hidden, grad_next], axis=1), (("height", 2),), 1)
    grad_acts = conv_taps(patches(grad_wide), flipped(weight_one), inputs.shape)
    flat_one = kernel_grad(acts_taps, grad_hidden)
    _, pull_norm_one = jax.vjp(norm_act, inputs, gain_one)
    grad_part, gain_one_part = pull_norm_one(grad_acts)
    grad_inputs = cotangent + grad_part
    channels = flat_one.shape[1]
    taps = flat_one.shape[0]
    count = (
        inputs.shape[0]
        * frames
        * rows
        * inputs.shape[3]
        * lax.axis_size("tm")
        * lax.axis_size("height")
        * lax.axis_size("batch")
    )
    factor = 1.0 / math.sqrt(count)
    parts = lax.axis_size("tm")
    share = taps // parts
    early = jnp.stack(
        [jnp.sum(grad_hidden, axis=(0, 1, 2, 3)), jnp.sum(cotangent, axis=(0, 1, 2, 3)), gain_two_part]
    )
    packed_two = jnp.concatenate(
        [flat_two.reshape(parts, share, channels), jnp.broadcast_to(early, (parts,) + early.shape)], axis=1
    )
    part_two = lax.psum(lax.psum_scatter(packed_two * factor, "tm", scatter_dimension=0), ("height", "batch"))
    packed_one = jnp.concatenate(
        [flat_one.reshape(parts, share, channels), jnp.broadcast_to(gain_one_part, (parts, 1, channels))], axis=1
    )
    part_one = reduced(packed_one * factor)
    vectors = jnp.concatenate([part_two[share : share + 2], part_one[share:], part_two[share + 2 :]])
    return (grad_inputs, part_one[:share], part_two[:share], vectors)


def solution(mesh):
    placed = (
        P("batch", "tm", "height", None, None),
        P(),
        P(),
        P(),
        P(),
        P(),
        P("batch", "tm", "height", None, None),
    )
    return jax.shard_map(
        on_device,
        mesh=mesh,
        in_specs=placed,
        out_specs=(P("batch", "tm", "height", None, None), P("tm", None), P("tm", None), P()),
        check_vma=False,
    )
```

```python
import math

import jax
import jax.numpy as jnp
from jax import lax
from jax.sharding import PartitionSpec as P


def passed_along(block, axis, distance):
    devices = range(lax.axis_size(axis))
    route = [(i - distance, i) for i in devices if i - distance in devices]
    return lax.ppermute(block, axis, route)


def padded(block, sides, width):
    for axis, dim in sides:
        count = lax.axis_size(axis)
        top = lax.slice_in_dim(block, block.shape[dim] - width, None, axis=dim)
        bottom = lax.slice_in_dim(block, 0, width, axis=dim)
        if count == 2:
            first = lax.axis_index(axis) == 0
            got = lax.ppermute(jnp.where(first, top, bottom), axis, [(0, 1), (1, 0)])
            empty = jnp.zeros_like(got)
            low = jnp.where(first, empty, got)
            high = jnp.where(first, got, empty)
        else:
            forward = [(i, i + 1) for i in range(count - 1)]
            backward = [(target, source) for source, target in forward]
            low = lax.ppermute(top, axis, forward)
            high = lax.ppermute(bottom, axis, backward)
        block = jnp.concatenate([low, block, high], axis=dim)
    return block


def norm_act(values, scales):
    square = jnp.mean(values * values, axis=-1, keepdims=True)
    return jax.nn.silu(values * lax.rsqrt(square + 1e-06) * scales)


def row_patches(wide):
    frames = wide.shape[1] - 2
    rows = wide.shape[2] - 2
    edged = jnp.pad(wide, ((0, 0), (0, 0), (0, 0), (1, 1), (0, 0)))
    pieces = [edged[:, i : i + frames, j : j + rows] for i in range(3) for j in range(3)]
    taps = jnp.concatenate(pieces, axis=-1)
    return taps.reshape(-1, taps.shape[-1])


def conv_rows(taps, kernel, shape):
    cols = shape[3]
    width = kernel.shape[-1]
    stacked = jnp.concatenate([kernel[:, :, l].reshape(-1, width) for l in range(3)], axis=1)
    out = jnp.dot(taps, stacked, precision=lax.Precision.HIGH)
    out = out.reshape(tuple(shape[:3]) + (cols + 2, 3 * width))
    return sum(out[:, :, :, l : l + cols, l * width : (l + 1) * width] for l in range(3))


def shifted_columns(values):
    return jnp.concatenate(
        [jnp.pad(values, ((0, 0), (0, 0), (0, 0), (l, 2 - l), (0, 0))) for l in range(3)], axis=-1
    )


def kernel_grad_rows(taps, grad):
    width = grad.shape[-1]
    flat = lax.optimization_barrier(shifted_columns(grad).reshape(-1, 3 * width).T)
    spread = lax.optimization_barrier(jnp.dot(flat, taps, precision=lax.Precision.HIGH))
    spread = spread.reshape(3, width, 3, 3, -1)
    return jnp.transpose(spread, (2, 3, 0, 4, 1)).reshape(-1, width)


def kernel_grad_rows_flipped(values, taps):
    channels = values.shape[-1]
    flat = lax.optimization_barrier(shifted_columns(values).reshape(-1, 3 * channels).T)
    spread = lax.optimization_barrier(jnp.dot(flat, taps, precision=lax.Precision.HIGH))
    spread = spread.reshape(3, channels, 3, 3, -1)[::-1, :, ::-1, ::-1]
    return jnp.transpose(spread, (2, 3, 0, 1, 4)).reshape(27 * channels, -1)


def flipped(kernel):
    return jnp.swapaxes(kernel[::-1, ::-1, ::-1], 3, 4)


def exchanged(block, axis, bit):
    count = lax.axis_size(axis)
    return lax.ppermute(block, axis, [(i, i ^ bit) for i in range(count)])


def halved(blocks, axis):
    count = lax.axis_size(axis)
    if count & (count - 1):
        return lax.psum_scatter(blocks, axis, scatter_dimension=0)
    me = lax.axis_index(axis)
    bit = 1
    while bit < count:
        mine = (me // bit) % 2
        pairs = blocks.reshape((blocks.shape[0] // 2, 2) + blocks.shape[1:])
        keep = lax.dynamic_index_in_dim(pairs, mine, axis=1, keepdims=False)
        send = lax.dynamic_index_in_dim(pairs, 1 - mine, axis=1, keepdims=False)
        blocks = keep + exchanged(send, axis, bit)
        bit *= 2
    return blocks[0]


def summed(block, axis):
    count = lax.axis_size(axis)
    if count & (count - 1):
        return lax.psum(block, axis)
    bit = 1
    while bit < count:
        block = block + exchanged(block, axis, bit)
        bit *= 2
    return block


def gathered(block, axis):
    count = lax.axis_size(axis)
    if count & (count - 1):
        return lax.all_gather(block, axis, tiled=True)
    me = lax.axis_index(axis)
    bit = 1
    while bit < count:
        other = exchanged(block, axis, bit)
        low = (me // bit) % 2 == 0
        block = jnp.where(low, jnp.concatenate([block, other]), jnp.concatenate([other, block]))
        bit *= 2
    return block


def reduced(blocks):
    parts, size, channels = blocks.shape
    split = lax.axis_size("height")
    width = -(-size // split)
    blocks = jnp.pad(blocks, ((0, 0), (0, width * split - size), (0, 0)))
    blocks = jnp.swapaxes(blocks.reshape(parts, split, width, channels), 0, 1)
    block = halved(halved(blocks, "height"), "tm")
    return gathered(summed(block, "batch"), "height")[:size]


def on_device(inputs, weight_one, bias_one, gain_one, weight_two, gain_two, cotangent):
    frames = inputs.shape[1]
    rows = inputs.shape[2]
    acts = norm_act(inputs, gain_one)
    acts_past = passed_along(acts[:, frames - 2 :], "tm", 1)
    cot_next = passed_along(cotangent[:, :2], "tm", -1)
    both = jnp.concatenate(
        [jnp.concatenate([acts_past, acts], axis=1), jnp.concatenate([cotangent, cot_next], axis=1)]
    )
    both = padded(both, (("height", 2),), 1)
    acts_wide = both[: inputs.shape[0]]
    cot_wide = both[inputs.shape[0] :]
    acts_taps = row_patches(acts_wide)
    hidden = conv_rows(acts_taps, weight_one, inputs.shape) + bias_one
    gated = norm_act(hidden, gain_two)
    cot_taps = row_patches(cot_wide)
    grad_gated = conv_rows(cot_taps, flipped(weight_two), inputs.shape)
    flat_two = kernel_grad_rows_flipped(gated, cot_taps)
    _, pull_norm_two = jax.vjp(norm_act, hidden, gain_two)
    grad_hidden, gain_two_part = pull_norm_two(grad_gated)
    grad_next = passed_along(grad_hidden[:, :2], "tm", -1)
    grad_wide = padded(jnp.concatenate([grad_hidden, grad_next], axis=1), (("height", 2),), 1)
    grad_acts = conv_rows(row_patches(grad_wide), flipped(weight_one), inputs.shape)
    flat_one = kernel_grad_rows(acts_taps, grad_hidden)
    _, pull_norm_one = jax.vjp(norm_act, inputs, gain_one)
    grad_part, gain_one_part = pull_norm_one(grad_acts)
    grad_inputs = cotangent + grad_part
    channels = flat_one.shape[1]
    taps = flat_one.shape[0]
    count = (
        inputs.shape[0]
        * frames
        * rows
        * inputs.shape[3]
        * lax.axis_size("tm")
        * lax.axis_size("height")
        * lax.axis_size("batch")
    )
    factor = 1.0 / math.sqrt(count)
    parts = lax.axis_size("tm")
    share = taps // parts
    vectors = jnp.stack(
        [
            jnp.sum(grad_hidden, axis=(0, 1, 2, 3)),
            jnp.sum(cotangent, axis=(0, 1, 2, 3)),
            gain_one_part,
            gain_two_part,
        ]
    )
    packed = jnp.concatenate(
        [
            flat_one.reshape(parts, share, channels),
            flat_two.reshape(parts, share, channels),
            jnp.broadcast_to(vectors, (parts,) + vectors.shape),
        ],
        axis=1,
    )
    total = reduced(packed * factor)
    return (grad_inputs, total[:share], total[share : 2 * share], total[2 * share :])


def solution(mesh):
    placed = (
        P("batch", "tm", "height", None, None),
        P(),
        P(),
        P(),
        P(),
        P(),
        P("batch", "tm", "height", None, None),
    )
    return jax.shard_map(
        on_device,
        mesh=mesh,
        in_specs=placed,
        out_specs=(P("batch", "tm", "height", None, None), P("tm", None), P("tm", None), P()),
        check_vma=False,
    )
```

```python
import math

import jax
import jax.numpy as jnp
from jax import lax
from jax.sharding import PartitionSpec as P


def passed_along(block, axis, distance):
    devices = range(lax.axis_size(axis))
    route = [(i - distance, i) for i in devices if i - distance in devices]
    return lax.ppermute(block, axis, route)


def padded(block, sides, width):
    for axis, dim in sides:
        count = lax.axis_size(axis)
        top = lax.slice_in_dim(block, block.shape[dim] - width, None, axis=dim)
        bottom = lax.slice_in_dim(block, 0, width, axis=dim)
        if count == 2:
            first = lax.axis_index(axis) == 0
            got = lax.ppermute(jnp.where(first, top, bottom), axis, [(0, 1), (1, 0)])
            empty = jnp.zeros_like(got)
            low = jnp.where(first, empty, got)
            high = jnp.where(first, got, empty)
        else:
            forward = [(i, i + 1) for i in range(count - 1)]
            backward = [(target, source) for source, target in forward]
            low = lax.ppermute(top, axis, forward)
            high = lax.ppermute(bottom, axis, backward)
        block = jnp.concatenate([low, block, high], axis=dim)
    return block


def norm_act(values, scales):
    square = jnp.mean(values * values, axis=-1, keepdims=True)
    return jax.nn.silu(values * lax.rsqrt(square + 1e-06) * scales)


def row_patches(wide, order=(0, 1, 2)):
    frames = wide.shape[1] - 2
    rows = wide.shape[2] - 2
    extra = -(wide.shape[3] + 2) % 8
    edged = jnp.pad(wide, ((0, 0), (0, 0), (0, 0), (1, 1 + extra), (0, 0)))
    pieces = [edged[:, i : i + frames, j : j + rows] for i in order for j in order]
    taps = jnp.concatenate(pieces, axis=-1)
    return taps.reshape(-1, taps.shape[-1])


def conv_rows(taps, kernel, shape):
    cols = shape[3]
    width = kernel.shape[-1]
    stacked = jnp.concatenate([kernel[:, :, l].reshape(-1, width) for l in range(3)], axis=1)
    out = jnp.dot(taps, stacked, precision=lax.Precision.HIGH)
    out = out.reshape(tuple(shape[:3]) + (-1, 3 * width))
    return sum(out[:, :, :, l : l + cols, l * width : (l + 1) * width] for l in range(3))


def shifted_columns(values, order=(0, 1, 2)):
    extra = -(values.shape[3] + 2) % 8
    return jnp.concatenate(
        [jnp.pad(values, ((0, 0), (0, 0), (0, 0), (l, 2 - l + extra), (0, 0))) for l in order], axis=-1
    )


def kernel_grad_rows(taps, grad, order=(0, 1, 2)):
    width = grad.shape[-1]
    flat = lax.optimization_barrier(shifted_columns(grad, order).reshape(-1, 3 * width).T)
    spread = lax.optimization_barrier(jnp.dot(flat, taps, precision=lax.Precision.HIGH))
    spread = spread.reshape(3, width, 3, 3, -1)
    return spread, width


def kernel_grad_forward(taps, grad):
    spread, width = kernel_grad_rows(taps, grad)
    return jnp.transpose(spread, (2, 3, 0, 4, 1)).reshape(-1, width)


def kernel_grad_reversed(values, taps):
    spread, channels = kernel_grad_rows(taps, values, (2, 1, 0))
    return jnp.transpose(spread, (2, 3, 0, 1, 4)).reshape(27 * channels, -1)


def mirrored(kernel):
    return jnp.swapaxes(kernel[:, :, ::-1], 3, 4)


def exchanged(block, axis, bit):
    count = lax.axis_size(axis)
    return lax.ppermute(block, axis, [(i, i ^ bit) for i in range(count)])


def halved(blocks, axis):
    count = lax.axis_size(axis)
    if count & (count - 1):
        return lax.psum_scatter(blocks, axis, scatter_dimension=0)
    me = lax.axis_index(axis)
    bit = 1
    while bit < count:
        mine = (me // bit) % 2
        pairs = blocks.reshape((blocks.shape[0] // 2, 2) + blocks.shape[1:])
        keep = lax.dynamic_index_in_dim(pairs, mine, axis=1, keepdims=False)
        send = lax.dynamic_index_in_dim(pairs, 1 - mine, axis=1, keepdims=False)
        blocks = keep + exchanged(send, axis, bit)
        bit *= 2
    return blocks[0]


def summed(block, axis):
    count = lax.axis_size(axis)
    if count & (count - 1):
        return lax.psum(block, axis)
    bit = 1
    while bit < count:
        block = block + exchanged(block, axis, bit)
        bit *= 2
    return block


def gathered(block, axis):
    count = lax.axis_size(axis)
    if count & (count - 1):
        return lax.all_gather(block, axis, tiled=True)
    me = lax.axis_index(axis)
    bit = 1
    while bit < count:
        other = exchanged(block, axis, bit)
        low = (me // bit) % 2 == 0
        block = jnp.where(low, jnp.concatenate([block, other]), jnp.concatenate([other, block]))
        bit *= 2
    return block


def reduced(blocks):
    parts, size, channels = blocks.shape
    split = lax.axis_size("height")
    width = -(-size // split)
    blocks = jnp.pad(blocks, ((0, 0), (0, width * split - size), (0, 0)))
    blocks = jnp.swapaxes(blocks.reshape(parts, split, width, channels), 0, 1)
    block = halved(halved(blocks, "height"), "tm")
    return gathered(summed(block, "batch"), "height")[:size]


def on_device(inputs, weight_one, bias_one, gain_one, weight_two, gain_two, cotangent):
    frames = inputs.shape[1]
    rows = inputs.shape[2]
    acts = norm_act(inputs, gain_one)
    acts_past = passed_along(acts[:, frames - 2 :], "tm", 1)
    cot_next = passed_along(cotangent[:, :2], "tm", -1)
    both = jnp.concatenate(
        [jnp.concatenate([acts_past, acts], axis=1), jnp.concatenate([cotangent, cot_next], axis=1)]
    )
    both = padded(both, (("height", 2),), 1)
    acts_wide = both[: inputs.shape[0]]
    cot_wide = both[inputs.shape[0] :]
    acts_taps = row_patches(acts_wide)
    hidden = conv_rows(acts_taps, weight_one, inputs.shape) + bias_one
    gated = norm_act(hidden, gain_two)
    cot_taps = row_patches(cot_wide, (2, 1, 0))
    grad_gated = conv_rows(cot_taps, mirrored(weight_two), inputs.shape)
    flat_two = kernel_grad_reversed(gated, cot_taps)
    _, pull_norm_two = jax.vjp(norm_act, hidden, gain_two)
    grad_hidden, gain_two_part = pull_norm_two(grad_gated)
    grad_next = passed_along(grad_hidden[:, :2], "tm", -1)
    grad_wide = padded(jnp.concatenate([grad_hidden, grad_next], axis=1), (("height", 2),), 1)
    grad_acts = conv_rows(row_patches(grad_wide, (2, 1, 0)), mirrored(weight_one), inputs.shape)
    flat_one = kernel_grad_forward(acts_taps, grad_hidden)
    _, pull_norm_one = jax.vjp(norm_act, inputs, gain_one)
    grad_part, gain_one_part = pull_norm_one(grad_acts)
    grad_inputs = cotangent + grad_part
    channels = flat_one.shape[1]
    taps = flat_one.shape[0]
    count = (
        inputs.shape[0]
        * frames
        * rows
        * inputs.shape[3]
        * lax.axis_size("tm")
        * lax.axis_size("height")
        * lax.axis_size("batch")
    )
    factor = 1.0 / math.sqrt(count)
    parts = lax.axis_size("tm")
    share = taps // parts
    vectors = jnp.stack(
        [
            jnp.sum(grad_hidden, axis=(0, 1, 2, 3)),
            jnp.sum(cotangent, axis=(0, 1, 2, 3)),
            gain_one_part,
            gain_two_part,
        ]
    )
    packed = jnp.concatenate(
        [
            flat_one.reshape(parts, share, channels),
            flat_two.reshape(parts, share, channels),
            jnp.broadcast_to(vectors, (parts,) + vectors.shape),
        ],
        axis=1,
    )
    total = reduced(packed * factor)
    return (grad_inputs, total[:share], total[share : 2 * share], total[2 * share :])


def solution(mesh):
    placed = (
        P("batch", "tm", "height", None, None),
        P(),
        P(),
        P(),
        P(),
        P(),
        P("batch", "tm", "height", None, None),
    )
    return jax.shard_map(
        on_device,
        mesh=mesh,
        in_specs=placed,
        out_specs=(P("batch", "tm", "height", None, None), P("tm", None), P("tm", None), P()),
        check_vma=False,
    )
```

```python
import math

import jax
import jax.numpy as jnp
from jax import lax
from jax.sharding import PartitionSpec as P


def passed_along(block, axis, distance):
    devices = range(lax.axis_size(axis))
    route = [(i - distance, i) for i in devices if i - distance in devices]
    return lax.ppermute(block, axis, route)


def padded(block, sides, width):
    for axis, dim in sides:
        count = lax.axis_size(axis)
        top = lax.slice_in_dim(block, block.shape[dim] - width, None, axis=dim)
        bottom = lax.slice_in_dim(block, 0, width, axis=dim)
        if count == 2:
            first = lax.axis_index(axis) == 0
            got = lax.ppermute(jnp.where(first, top, bottom), axis, [(0, 1), (1, 0)])
            empty = jnp.zeros_like(got)
            low = jnp.where(first, empty, got)
            high = jnp.where(first, got, empty)
        else:
            forward = [(i, i + 1) for i in range(count - 1)]
            backward = [(target, source) for source, target in forward]
            low = lax.ppermute(top, axis, forward)
            high = lax.ppermute(bottom, axis, backward)
        block = jnp.concatenate([low, block, high], axis=dim)
    return block


def norm_act(values, scales):
    square = jnp.mean(values * values, axis=-1, keepdims=True)
    return jax.nn.silu(values * lax.rsqrt(square + 1e-06) * scales)


def row_patches(wide, order=(0, 1, 2)):
    frames = wide.shape[1] - 2
    rows = wide.shape[2] - 2
    extra = -(wide.shape[3] + 2) % 8
    edged = jnp.pad(wide, ((0, 0), (0, 0), (0, 0), (1, 1 + extra), (0, 0)))
    pieces = [edged[:, i : i + frames, j : j + rows] for i in order for j in order]
    taps = jnp.concatenate(pieces, axis=-1)
    return taps.reshape(-1, taps.shape[-1])


def conv_rows(taps, kernel, shape):
    cols = shape[3]
    width = kernel.shape[-1]
    stacked = jnp.transpose(kernel, (0, 1, 3, 2, 4)).reshape(-1, 3 * width)
    out = jnp.dot(taps, stacked, precision=lax.Precision.HIGH)
    out = out.reshape(tuple(shape[:3]) + (-1, 3 * width))
    return sum(out[:, :, :, l : l + cols, l * width : (l + 1) * width] for l in range(3))


def shifted_columns(values, order=(0, 1, 2)):
    extra = -(values.shape[3] + 2) % 8
    return jnp.concatenate(
        [jnp.pad(values, ((0, 0), (0, 0), (0, 0), (l, 2 - l + extra), (0, 0))) for l in order], axis=-1
    )


def kernel_grad_rows(taps, grad, order=(0, 1, 2)):
    width = grad.shape[-1]
    flat = lax.optimization_barrier(shifted_columns(grad, order).reshape(-1, 3 * width).T)
    spread = lax.optimization_barrier(jnp.dot(flat, taps, precision=lax.Precision.HIGH))
    spread = spread.reshape(3, width, 3, 3, -1)
    return spread, width


def kernel_grad_forward(taps, grad):
    spread, width = kernel_grad_rows(taps, grad)
    return jnp.transpose(spread, (2, 3, 0, 4, 1)).reshape(-1, width)


def kernel_grad_reversed(values, taps):
    spread, channels = kernel_grad_rows(taps, values, (2, 1, 0))
    return jnp.transpose(spread, (2, 3, 0, 1, 4)).reshape(27 * channels, -1)


def mirrored(kernel):
    return jnp.swapaxes(kernel[:, :, ::-1], 3, 4)


def exchanged(block, axis, bit):
    count = lax.axis_size(axis)
    return lax.ppermute(block, axis, [(i, i ^ bit) for i in range(count)])


def halved(blocks, axis):
    count = lax.axis_size(axis)
    if count & (count - 1):
        return lax.psum_scatter(blocks, axis, scatter_dimension=0)
    me = lax.axis_index(axis)
    bit = 1
    while bit < count:
        mine = (me // bit) % 2
        pairs = blocks.reshape((blocks.shape[0] // 2, 2) + blocks.shape[1:])
        keep = lax.dynamic_index_in_dim(pairs, mine, axis=1, keepdims=False)
        send = lax.dynamic_index_in_dim(pairs, 1 - mine, axis=1, keepdims=False)
        blocks = keep + exchanged(send, axis, bit)
        bit *= 2
    return blocks[0]


def summed(block, axis):
    count = lax.axis_size(axis)
    if count & (count - 1):
        return lax.psum(block, axis)
    bit = 1
    while bit < count:
        block = block + exchanged(block, axis, bit)
        bit *= 2
    return block


def gathered(block, axis):
    count = lax.axis_size(axis)
    if count & (count - 1):
        return lax.all_gather(block, axis, tiled=True)
    me = lax.axis_index(axis)
    bit = 1
    while bit < count:
        other = exchanged(block, axis, bit)
        low = (me // bit) % 2 == 0
        block = jnp.where(low, jnp.concatenate([block, other]), jnp.concatenate([other, block]))
        bit *= 2
    return block


def reduced(blocks):
    parts, size, channels = blocks.shape
    split = lax.axis_size("height")
    width = -(-size // split)
    blocks = jnp.pad(blocks, ((0, 0), (0, width * split - size), (0, 0)))
    blocks = jnp.swapaxes(blocks.reshape(parts, split, width, channels), 0, 1)
    block = halved(halved(blocks, "height"), "tm")
    return gathered(summed(block, "batch"), "height")[:size]


def on_device(inputs, weight_one, bias_one, gain_one, weight_two, gain_two, cotangent):
    frames = inputs.shape[1]
    rows = inputs.shape[2]
    acts = norm_act(inputs, gain_one)
    acts_past = passed_along(acts[:, frames - 2 :], "tm", 1)
    cot_next = passed_along(cotangent[:, :2], "tm", -1)
    both = jnp.concatenate(
        [jnp.concatenate([acts_past, acts], axis=1), jnp.concatenate([cotangent, cot_next], axis=1)]
    )
    both = padded(both, (("height", 2),), 1)
    acts_wide = both[: inputs.shape[0]]
    cot_wide = both[inputs.shape[0] :]
    acts_taps = row_patches(acts_wide)
    hidden = conv_rows(acts_taps, weight_one, inputs.shape) + bias_one
    gated = norm_act(hidden, gain_two)
    cot_taps = row_patches(cot_wide, (2, 1, 0))
    grad_gated = conv_rows(cot_taps, mirrored(weight_two), inputs.shape)
    flat_two = kernel_grad_reversed(gated, cot_taps)
    _, pull_norm_two = jax.vjp(norm_act, hidden, gain_two)
    grad_hidden, gain_two_part = pull_norm_two(grad_gated)
    grad_next = passed_along(grad_hidden[:, :2], "tm", -1)
    grad_wide = padded(jnp.concatenate([grad_hidden, grad_next], axis=1), (("height", 2),), 1)
    grad_acts = conv_rows(row_patches(grad_wide, (2, 1, 0)), mirrored(weight_one), inputs.shape)
    flat_one = kernel_grad_forward(acts_taps, grad_hidden)
    _, pull_norm_one = jax.vjp(norm_act, inputs, gain_one)
    grad_part, gain_one_part = pull_norm_one(grad_acts)
    grad_inputs = cotangent + grad_part
    channels = flat_one.shape[1]
    taps = flat_one.shape[0]
    count = (
        inputs.shape[0]
        * frames
        * rows
        * inputs.shape[3]
        * lax.axis_size("tm")
        * lax.axis_size("height")
        * lax.axis_size("batch")
    )
    factor = 1.0 / math.sqrt(count)
    parts = lax.axis_size("tm")
    share = taps // parts
    vectors = jnp.stack(
        [
            jnp.sum(grad_hidden, axis=(0, 1, 2, 3)),
            jnp.sum(cotangent, axis=(0, 1, 2, 3)),
            gain_one_part,
            gain_two_part,
        ]
    )
    packed = jnp.concatenate(
        [
            flat_one.reshape(parts, share, channels),
            flat_two.reshape(parts, share, channels),
            jnp.broadcast_to(vectors, (parts,) + vectors.shape),
        ],
        axis=1,
    )
    total = reduced(packed * factor)
    return (grad_inputs, total[:share], total[share : 2 * share], total[2 * share :])


def solution(mesh):
    placed = (
        P("batch", "tm", "height", None, None),
        P(),
        P(),
        P(),
        P(),
        P(),
        P("batch", "tm", "height", None, None),
    )
    return jax.shard_map(
        on_device,
        mesh=mesh,
        in_specs=placed,
        out_specs=(P("batch", "tm", "height", None, None), P("tm", None), P("tm", None), P()),
        check_vma=False,
    )
```

```python
import math

import jax
import jax.numpy as jnp
from jax import lax
from jax.sharding import PartitionSpec as P


def passed_along(block, axis, distance):
    devices = range(lax.axis_size(axis))
    route = [(i - distance, i) for i in devices if i - distance in devices]
    return lax.ppermute(block, axis, route)


def padded(block, sides, width):
    for axis, dim in sides:
        count = lax.axis_size(axis)
        top = lax.slice_in_dim(block, block.shape[dim] - width, None, axis=dim)
        bottom = lax.slice_in_dim(block, 0, width, axis=dim)
        if count == 2:
            first = lax.axis_index(axis) == 0
            got = lax.ppermute(jnp.where(first, top, bottom), axis, [(0, 1), (1, 0)])
            empty = jnp.zeros_like(got)
            low = jnp.where(first, empty, got)
            high = jnp.where(first, got, empty)
        else:
            forward = [(i, i + 1) for i in range(count - 1)]
            backward = [(target, source) for source, target in forward]
            low = lax.ppermute(top, axis, forward)
            high = lax.ppermute(bottom, axis, backward)
        block = jnp.concatenate([low, block, high], axis=dim)
    return block


def norm_act(values, scales):
    square = jnp.mean(values * values, axis=-1, keepdims=True)
    return jax.nn.silu(values * lax.rsqrt(square + 1e-06) * scales)


def row_patches(wide, order=(0, 1, 2)):
    frames = wide.shape[1] - 2
    rows = wide.shape[2] - 2
    extra = -(wide.shape[3] + 2) % 8
    edged = jnp.pad(wide, ((0, 0), (0, 0), (0, 0), (1, 1 + extra), (0, 0)))
    pieces = [edged[:, i : i + frames, j : j + rows] for i in order for j in order]
    taps = jnp.concatenate(pieces, axis=-1)
    return taps.reshape(-1, taps.shape[-1])


def conv_rows(taps, kernel, shape):
    cols = shape[3]
    width = kernel.shape[-1]
    stacked = jnp.transpose(kernel, (0, 1, 3, 2, 4)).reshape(-1, 3 * width)
    out = jnp.dot(taps, stacked, precision=lax.Precision.HIGH)
    out = out.reshape(tuple(shape[:3]) + (-1, 3 * width))
    return sum(out[:, :, :, l : l + cols, l * width : (l + 1) * width] for l in range(3))


def shifted_columns(values, order=(0, 1, 2)):
    extra = -(values.shape[3] + 2) % 8
    return jnp.concatenate(
        [jnp.pad(values, ((0, 0), (0, 0), (0, 0), (l, 2 - l + extra), (0, 0))) for l in order], axis=-1
    )


def kernel_grad_rows(taps, grad, order=(0, 1, 2)):
    width = grad.shape[-1]
    flat = lax.optimization_barrier(shifted_columns(grad, order).reshape(-1, 3 * width).T)
    spread = lax.optimization_barrier(jnp.dot(flat, taps, precision=lax.Precision.HIGH))
    spread = spread.reshape(3, width, 3, 3, -1)
    return spread, width


def kernel_grad_forward(taps, grad):
    spread, width = kernel_grad_rows(taps, grad)
    return jnp.transpose(spread, (2, 3, 0, 4, 1)).reshape(-1, width)


def kernel_grad_reversed(values, taps):
    spread, channels = kernel_grad_rows(taps, values, (2, 1, 0))
    return jnp.transpose(spread, (2, 3, 0, 1, 4)).reshape(27 * channels, -1)


def mirrored(kernel):
    return jnp.swapaxes(kernel[:, :, ::-1], 3, 4)


def exchanged(block, axis, bit):
    count = lax.axis_size(axis)
    return lax.ppermute(block, axis, [(i, i ^ bit) for i in range(count)])


def halved(blocks, axis):
    count = lax.axis_size(axis)
    if count & (count - 1):
        return lax.psum_scatter(blocks, axis, scatter_dimension=0)
    me = lax.axis_index(axis)
    bit = 1
    while bit < count:
        mine = (me // bit) % 2
        pairs = blocks.reshape((blocks.shape[0] // 2, 2) + blocks.shape[1:])
        keep = lax.dynamic_index_in_dim(pairs, mine, axis=1, keepdims=False)
        send = lax.dynamic_index_in_dim(pairs, 1 - mine, axis=1, keepdims=False)
        blocks = keep + exchanged(send, axis, bit)
        bit *= 2
    return blocks[0]


def swapped_low(t):
    return t - t % 4 + (t % 2) * 2 + (t // 2) % 2


def halved_across(blocks):
    count = lax.axis_size("tm")
    heights = lax.axis_size("height")
    if count & (count - 1) or count < 4 or heights < 2:
        return halved(blocks, "tm")
    odd = lax.axis_index("height") % 2 == 1
    order = [swapped_low(k) for k in range(count)]
    blocks = jnp.where(odd, jnp.stack([blocks[k] for k in order]), blocks)
    me = lax.axis_index("tm")
    label = jnp.where(odd, swapped_low(me), me)
    bit = 1
    while bit < count:
        mine = (label // bit) % 2
        pairs = blocks.reshape((blocks.shape[0] // 2, 2) + blocks.shape[1:])
        keep = lax.dynamic_index_in_dim(pairs, mine, axis=1, keepdims=False)
        send = lax.dynamic_index_in_dim(pairs, 1 - mine, axis=1, keepdims=False)
        route = []
        for t in range(count):
            for h in range(heights):
                relabel = swapped_low if h % 2 else (lambda v: v)
                route.append((t * heights + h, relabel(relabel(t) ^ bit) * heights + h))
        blocks = keep + lax.ppermute(send, ("tm", "height"), route)
        bit *= 2
    return blocks[0]


def summed(block, axis):
    count = lax.axis_size(axis)
    if count & (count - 1):
        return lax.psum(block, axis)
    bit = 1
    while bit < count:
        block = block + exchanged(block, axis, bit)
        bit *= 2
    return block


def gathered(block, axis):
    count = lax.axis_size(axis)
    if count & (count - 1):
        return lax.all_gather(block, axis, tiled=True)
    me = lax.axis_index(axis)
    bit = 1
    while bit < count:
        other = exchanged(block, axis, bit)
        low = (me // bit) % 2 == 0
        block = jnp.where(low, jnp.concatenate([block, other]), jnp.concatenate([other, block]))
        bit *= 2
    return block


def reduced(blocks):
    parts, size, channels = blocks.shape
    split = lax.axis_size("height")
    width = -(-size // split)
    blocks = jnp.pad(blocks, ((0, 0), (0, width * split - size), (0, 0)))
    blocks = jnp.swapaxes(blocks.reshape(parts, split, width, channels), 0, 1)
    block = halved_across(halved(blocks, "height"))
    return gathered(summed(block, "batch"), "height")[:size]


def on_device(inputs, weight_one, bias_one, gain_one, weight_two, gain_two, cotangent):
    frames = inputs.shape[1]
    rows = inputs.shape[2]
    acts = norm_act(inputs, gain_one)
    acts_past = passed_along(acts[:, frames - 2 :], "tm", 1)
    cot_next = passed_along(cotangent[:, :2], "tm", -1)
    both = jnp.concatenate(
        [jnp.concatenate([acts_past, acts], axis=1), jnp.concatenate([cotangent, cot_next], axis=1)]
    )
    both = padded(both, (("height", 2),), 1)
    acts_wide = both[: inputs.shape[0]]
    cot_wide = both[inputs.shape[0] :]
    acts_taps = row_patches(acts_wide)
    hidden = conv_rows(acts_taps, weight_one, inputs.shape) + bias_one
    gated = norm_act(hidden, gain_two)
    cot_taps = row_patches(cot_wide, (2, 1, 0))
    grad_gated = conv_rows(cot_taps, mirrored(weight_two), inputs.shape)
    flat_two = kernel_grad_reversed(gated, cot_taps)
    _, pull_norm_two = jax.vjp(norm_act, hidden, gain_two)
    grad_hidden, gain_two_part = pull_norm_two(grad_gated)
    grad_next = passed_along(grad_hidden[:, :2], "tm", -1)
    grad_wide = padded(jnp.concatenate([grad_hidden, grad_next], axis=1), (("height", 2),), 1)
    grad_acts = conv_rows(row_patches(grad_wide, (2, 1, 0)), mirrored(weight_one), inputs.shape)
    flat_one = kernel_grad_forward(acts_taps, grad_hidden)
    _, pull_norm_one = jax.vjp(norm_act, inputs, gain_one)
    grad_part, gain_one_part = pull_norm_one(grad_acts)
    grad_inputs = cotangent + grad_part
    channels = flat_one.shape[1]
    taps = flat_one.shape[0]
    count = (
        inputs.shape[0]
        * frames
        * rows
        * inputs.shape[3]
        * lax.axis_size("tm")
        * lax.axis_size("height")
        * lax.axis_size("batch")
    )
    factor = 1.0 / math.sqrt(count)
    parts = lax.axis_size("tm")
    share = taps // parts
    vectors = jnp.stack(
        [
            jnp.sum(grad_hidden, axis=(0, 1, 2, 3)),
            jnp.sum(cotangent, axis=(0, 1, 2, 3)),
            gain_one_part,
            gain_two_part,
        ]
    )
    packed = jnp.concatenate(
        [
            flat_one.reshape(parts, share, channels),
            flat_two.reshape(parts, share, channels),
            jnp.broadcast_to(vectors, (parts,) + vectors.shape),
        ],
        axis=1,
    )
    total = reduced(packed * factor)
    return (grad_inputs, total[:share], total[share : 2 * share], total[2 * share :])


def solution(mesh):
    placed = (
        P("batch", "tm", "height", None, None),
        P(),
        P(),
        P(),
        P(),
        P(),
        P("batch", "tm", "height", None, None),
    )
    return jax.shard_map(
        on_device,
        mesh=mesh,
        in_specs=placed,
        out_specs=(P("batch", "tm", "height", None, None), P("tm", None), P("tm", None), P()),
        check_vma=False,
    )
```

```python
import math

import jax
import jax.numpy as jnp
from jax import lax
from jax.sharding import PartitionSpec as P


def passed_along(block, axis, distance):
    devices = range(lax.axis_size(axis))
    route = [(i - distance, i) for i in devices if i - distance in devices]
    return lax.ppermute(block, axis, route)


def padded(block, sides, width):
    for axis, dim in sides:
        count = lax.axis_size(axis)
        top = lax.slice_in_dim(block, block.shape[dim] - width, None, axis=dim)
        bottom = lax.slice_in_dim(block, 0, width, axis=dim)
        if count == 2:
            first = lax.axis_index(axis) == 0
            got = lax.ppermute(jnp.where(first, top, bottom), axis, [(0, 1), (1, 0)])
            empty = jnp.zeros_like(got)
            low = jnp.where(first, empty, got)
            high = jnp.where(first, got, empty)
        else:
            forward = [(i, i + 1) for i in range(count - 1)]
            backward = [(target, source) for source, target in forward]
            low = lax.ppermute(top, axis, forward)
            high = lax.ppermute(bottom, axis, backward)
        block = jnp.concatenate([low, block, high], axis=dim)
    return block


def norm_act(values, scales):
    square = jnp.mean(values * values, axis=-1, keepdims=True)
    return jax.nn.silu(values * lax.rsqrt(square + 1e-06) * scales)


def row_patches(wide, order=(0, 1, 2)):
    frames = wide.shape[1] - 2
    rows = wide.shape[2] - 2
    extra = -(wide.shape[3] + 2) % 8
    edged = jnp.pad(wide, ((0, 0), (0, 0), (0, 0), (1, 1 + extra), (0, 0)))
    pieces = [edged[:, i : i + frames, j : j + rows] for i in order for j in order]
    taps = jnp.concatenate(pieces, axis=-1)
    return taps.reshape(-1, taps.shape[-1])


def conv_rows(taps, kernel, shape):
    cols = shape[3]
    width = kernel.shape[-1]
    stacked = jnp.transpose(kernel, (0, 1, 3, 2, 4)).reshape(-1, 3 * width)
    out = jnp.dot(taps, stacked, precision=lax.Precision.HIGH)
    out = out.reshape(tuple(shape[:3]) + (-1, 3 * width))
    return sum(out[:, :, :, l : l + cols, l * width : (l + 1) * width] for l in range(3))


def shifted_columns(values, order=(0, 1, 2)):
    extra = -(values.shape[3] + 2) % 8
    return jnp.concatenate(
        [jnp.pad(values, ((0, 0), (0, 0), (0, 0), (l, 2 - l + extra), (0, 0))) for l in order], axis=-1
    )


def kernel_grad_rows(taps, grad, order=(0, 1, 2)):
    width = grad.shape[-1]
    flat = lax.optimization_barrier(shifted_columns(grad, order).reshape(-1, 3 * width).T)
    spread = lax.optimization_barrier(jnp.dot(flat, taps, precision=lax.Precision.HIGH))
    spread = spread.reshape(3, width, 3, 3, -1)
    return spread, width


def kernel_grad_forward(taps, grad):
    spread, width = kernel_grad_rows(taps, grad)
    return jnp.transpose(spread, (2, 3, 0, 4, 1)).reshape(-1, width)


def kernel_grad_reversed(values, taps):
    spread, channels = kernel_grad_rows(taps, values, (2, 1, 0))
    return jnp.transpose(spread, (2, 3, 0, 1, 4)).reshape(27 * channels, -1)


def mirrored(kernel):
    return jnp.swapaxes(kernel[:, :, ::-1], 3, 4)


def exchanged(block, axis, bit):
    count = lax.axis_size(axis)
    return lax.ppermute(block, axis, [(i, i ^ bit) for i in range(count)])


def halved(blocks, axis):
    count = lax.axis_size(axis)
    if count & (count - 1):
        return lax.psum_scatter(blocks, axis, scatter_dimension=0)
    me = lax.axis_index(axis)
    bit = 1
    while bit < count:
        mine = (me // bit) % 2
        pairs = blocks.reshape((blocks.shape[0] // 2, 2) + blocks.shape[1:])
        keep = lax.dynamic_index_in_dim(pairs, mine, axis=1, keepdims=False)
        send = lax.dynamic_index_in_dim(pairs, 1 - mine, axis=1, keepdims=False)
        blocks = keep + exchanged(send, axis, bit)
        bit *= 2
    return blocks[0]


def swapped_low(t):
    return t - t % 4 + (t % 2) * 2 + (t // 2) % 2


def halved_across(blocks):
    count = lax.axis_size("tm")
    heights = lax.axis_size("height")
    if count & (count - 1) or count < 4 or heights < 2:
        return halved(blocks, "tm")
    odd = lax.axis_index("height") % 2 == 1
    order = [swapped_low(k) for k in range(count)]
    blocks = jnp.where(odd, jnp.stack([blocks[k] for k in order]), blocks)
    me = lax.axis_index("tm")
    label = jnp.where(odd, swapped_low(me), me)
    bit = 1
    while bit < count:
        mine = (label // bit) % 2
        pairs = blocks.reshape((blocks.shape[0] // 2, 2) + blocks.shape[1:])
        keep = lax.dynamic_index_in_dim(pairs, mine, axis=1, keepdims=False)
        send = lax.dynamic_index_in_dim(pairs, 1 - mine, axis=1, keepdims=False)
        route = []
        for t in range(count):
            for h in range(heights):
                relabel = swapped_low if h % 2 else (lambda v: v)
                route.append((t * heights + h, relabel(relabel(t) ^ bit) * heights + h))
        blocks = keep + lax.ppermute(send, ("tm", "height"), route)
        bit *= 2
    return blocks[0]


def summed(block, axis):
    count = lax.axis_size(axis)
    if count & (count - 1):
        return lax.psum(block, axis)
    bit = 1
    while bit < count:
        block = block + exchanged(block, axis, bit)
        bit *= 2
    return block


def gathered(block, axis):
    count = lax.axis_size(axis)
    if count & (count - 1):
        return lax.all_gather(block, axis, tiled=True)
    me = lax.axis_index(axis)
    bit = 1
    while bit < count:
        other = exchanged(block, axis, bit)
        low = (me // bit) % 2 == 0
        block = jnp.where(low, jnp.concatenate([block, other]), jnp.concatenate([other, block]))
        bit *= 2
    return block


def reduced(blocks):
    parts, size, channels = blocks.shape
    split = lax.axis_size("height")
    width = -(-size // split)
    blocks = jnp.pad(blocks, ((0, 0), (0, width * split - size), (0, 0)))
    blocks = jnp.swapaxes(blocks.reshape(parts, split, width, channels), 0, 1)
    block = halved_across(halved(blocks, "height"))
    return gathered(summed(block, "batch"), "height")[:size]


def on_device(inputs, weight_one, bias_one, gain_one, weight_two, gain_two, cotangent):
    frames = inputs.shape[1]
    rows = inputs.shape[2]
    acts = norm_act(inputs, gain_one)
    acts_past = norm_act(passed_along(inputs[:, frames - 2 :], "tm", 1), gain_one)
    cot_next = passed_along(cotangent[:, :2], "tm", -1)
    both = jnp.concatenate(
        [jnp.concatenate([acts_past, acts], axis=1), jnp.concatenate([cotangent, cot_next], axis=1)]
    )
    both = padded(both, (("height", 2),), 1)
    acts_wide = both[: inputs.shape[0]]
    cot_wide = both[inputs.shape[0] :]
    acts_taps = row_patches(acts_wide)
    hidden = conv_rows(acts_taps, weight_one, inputs.shape) + bias_one
    gated = norm_act(hidden, gain_two)
    cot_taps = row_patches(cot_wide, (2, 1, 0))
    grad_gated = conv_rows(cot_taps, mirrored(weight_two), inputs.shape)
    flat_two = kernel_grad_reversed(gated, cot_taps)
    _, pull_norm_two = jax.vjp(norm_act, hidden, gain_two)
    grad_hidden, gain_two_part = pull_norm_two(grad_gated)
    grad_next = passed_along(grad_hidden[:, :2], "tm", -1)
    grad_wide = padded(jnp.concatenate([grad_hidden, grad_next], axis=1), (("height", 2),), 1)
    grad_acts = conv_rows(row_patches(grad_wide, (2, 1, 0)), mirrored(weight_one), inputs.shape)
    flat_one = kernel_grad_forward(acts_taps, grad_hidden)
    _, pull_norm_one = jax.vjp(norm_act, inputs, gain_one)
    grad_part, gain_one_part = pull_norm_one(grad_acts)
    grad_inputs = cotangent + grad_part
    channels = flat_one.shape[1]
    taps = flat_one.shape[0]
    count = (
        inputs.shape[0]
        * frames
        * rows
        * inputs.shape[3]
        * lax.axis_size("tm")
        * lax.axis_size("height")
        * lax.axis_size("batch")
    )
    factor = 1.0 / math.sqrt(count)
    parts = lax.axis_size("tm")
    share = taps // parts
    vectors = jnp.stack(
        [
            jnp.sum(grad_hidden, axis=(0, 1, 2, 3)),
            jnp.sum(cotangent, axis=(0, 1, 2, 3)),
            gain_one_part,
            gain_two_part,
        ]
    )
    packed = jnp.concatenate(
        [
            flat_one.reshape(parts, share, channels),
            flat_two.reshape(parts, share, channels),
            jnp.broadcast_to(vectors, (parts,) + vectors.shape),
        ],
        axis=1,
    )
    total = reduced(packed * factor)
    return (grad_inputs, total[:share], total[share : 2 * share], total[2 * share :])


def solution(mesh):
    placed = (
        P("batch", "tm", "height", None, None),
        P(),
        P(),
        P(),
        P(),
        P(),
        P("batch", "tm", "height", None, None),
    )
    return jax.shard_map(
        on_device,
        mesh=mesh,
        in_specs=placed,
        out_specs=(P("batch", "tm", "height", None, None), P("tm", None), P("tm", None), P()),
        check_vma=False,
    )
```

```python
import math

import jax
import jax.numpy as jnp
from jax import lax
from jax.sharding import PartitionSpec as P


def passed_along(block, axis, distance):
    devices = range(lax.axis_size(axis))
    route = [(i - distance, i) for i in devices if i - distance in devices]
    return lax.ppermute(block, axis, route)


def padded(block, sides, width):
    for axis, dim in sides:
        count = lax.axis_size(axis)
        top = lax.slice_in_dim(block, block.shape[dim] - width, None, axis=dim)
        bottom = lax.slice_in_dim(block, 0, width, axis=dim)
        if count == 2:
            first = lax.axis_index(axis) == 0
            got = lax.ppermute(jnp.where(first, top, bottom), axis, [(0, 1), (1, 0)])
            empty = jnp.zeros_like(got)
            low = jnp.where(first, empty, got)
            high = jnp.where(first, got, empty)
        else:
            forward = [(i, i + 1) for i in range(count - 1)]
            backward = [(target, source) for source, target in forward]
            low = lax.ppermute(top, axis, forward)
            high = lax.ppermute(bottom, axis, backward)
        block = jnp.concatenate([low, block, high], axis=dim)
    return block


def norm_act(values, scales):
    square = jnp.mean(values * values, axis=-1, keepdims=True)
    return jax.nn.silu(values * lax.rsqrt(square + 1e-06) * scales)


def row_patches(wide, order=(0, 1, 2)):
    frames = wide.shape[1] - 2
    rows = wide.shape[2] - 2
    extra = -(wide.shape[3] + 2) % 8
    edged = jnp.pad(wide, ((0, 0), (0, 0), (0, 0), (1, 1 + extra), (0, 0)))
    pieces = [edged[:, i : i + frames, j : j + rows] for i in order for j in order]
    taps = jnp.concatenate(pieces, axis=-1)
    return taps.reshape(-1, taps.shape[-1])


def conv_rows(taps, kernel, shape):
    cols = shape[3]
    width = kernel.shape[-1]
    stacked = jnp.transpose(kernel, (0, 1, 3, 2, 4)).reshape(-1, 3 * width)
    out = jnp.dot(taps, stacked, precision=lax.Precision.HIGH)
    out = out.reshape(tuple(shape[:3]) + (-1, 3 * width))
    return sum(out[:, :, :, l : l + cols, l * width : (l + 1) * width] for l in range(3))


def shifted_columns(values, order=(0, 1, 2)):
    extra = -(values.shape[3] + 2) % 8
    return jnp.concatenate(
        [jnp.pad(values, ((0, 0), (0, 0), (0, 0), (l, 2 - l + extra), (0, 0))) for l in order], axis=-1
    )


def kernel_grad_rows(taps, grad, order=(0, 1, 2)):
    width = grad.shape[-1]
    flat = lax.optimization_barrier(shifted_columns(grad, order).reshape(-1, 3 * width).T)
    spread = lax.optimization_barrier(jnp.dot(flat, taps, precision=lax.Precision.HIGH))
    spread = spread.reshape(3, width, 3, 3, -1)
    return spread, width


def kernel_grad_forward(taps, grad):
    spread, width = kernel_grad_rows(taps, grad)
    return jnp.transpose(spread, (2, 3, 0, 4, 1)).reshape(-1, width)


def kernel_grad_reversed(values, taps):
    spread, channels = kernel_grad_rows(taps, values, (2, 1, 0))
    return jnp.transpose(spread, (2, 3, 0, 1, 4)).reshape(27 * channels, -1)


def mirrored(kernel):
    return jnp.swapaxes(kernel[:, :, ::-1], 3, 4)


def exchanged(block, axis, bit):
    count = lax.axis_size(axis)
    return lax.ppermute(block, axis, [(i, i ^ bit) for i in range(count)])


def halved(blocks, axis, dim=0):
    count = lax.axis_size(axis)
    if count & (count - 1):
        return lax.psum_scatter(blocks, axis, scatter_dimension=dim)
    me = lax.axis_index(axis)
    bit = 1
    while bit < count:
        mine = (me // bit) % 2
        shape = blocks.shape
        pairs = blocks.reshape(shape[:dim] + (shape[dim] // 2, 2) + shape[dim + 1 :])
        keep = lax.dynamic_index_in_dim(pairs, mine, axis=dim + 1, keepdims=False)
        send = lax.dynamic_index_in_dim(pairs, 1 - mine, axis=dim + 1, keepdims=False)
        blocks = keep + exchanged(send, axis, bit)
        bit *= 2
    return lax.index_in_dim(blocks, 0, dim, keepdims=False)


def swapped_low(t):
    return t - t % 4 + (t % 2) * 2 + (t // 2) % 2


def halved_across(blocks):
    count = lax.axis_size("tm")
    heights = lax.axis_size("height")
    if count & (count - 1) or count < 4 or heights < 2:
        return halved(blocks, "tm")
    odd = lax.axis_index("height") % 2 == 1
    order = [swapped_low(k) for k in range(count)]
    blocks = jnp.where(odd, jnp.stack([blocks[k] for k in order]), blocks)
    me = lax.axis_index("tm")
    label = jnp.where(odd, swapped_low(me), me)
    bit = 1
    while bit < count:
        mine = (label // bit) % 2
        pairs = blocks.reshape((blocks.shape[0] // 2, 2) + blocks.shape[1:])
        keep = lax.dynamic_index_in_dim(pairs, mine, axis=1, keepdims=False)
        send = lax.dynamic_index_in_dim(pairs, 1 - mine, axis=1, keepdims=False)
        route = []
        for t in range(count):
            for h in range(heights):
                relabel = swapped_low if h % 2 else (lambda v: v)
                route.append((t * heights + h, relabel(relabel(t) ^ bit) * heights + h))
        blocks = keep + lax.ppermute(send, ("tm", "height"), route)
        bit *= 2
    return blocks[0]


def summed(block, axis):
    count = lax.axis_size(axis)
    if count & (count - 1):
        return lax.psum(block, axis)
    bit = 1
    while bit < count:
        block = block + exchanged(block, axis, bit)
        bit *= 2
    return block


def gathered(block, axis):
    count = lax.axis_size(axis)
    if count & (count - 1):
        return lax.all_gather(block, axis, tiled=True)
    me = lax.axis_index(axis)
    bit = 1
    while bit < count:
        other = exchanged(block, axis, bit)
        low = (me // bit) % 2 == 0
        block = jnp.where(low, jnp.concatenate([block, other]), jnp.concatenate([other, block]))
        bit *= 2
    return block


def reduced(blocks):
    parts, size, channels = blocks.shape
    split = lax.axis_size("height")
    width = -(-size // split)
    blocks = jnp.pad(blocks, ((0, 0), (0, width * split - size), (0, 0)))
    blocks = blocks.reshape(parts, split, width, channels)
    block = halved_across(halved(blocks, "height", 1))
    return gathered(summed(block, "batch"), "height")[:size]


def on_device(inputs, weight_one, bias_one, gain_one, weight_two, gain_two, cotangent):
    frames = inputs.shape[1]
    rows = inputs.shape[2]
    acts = norm_act(inputs, gain_one)
    acts_past = passed_along(acts[:, frames - 2 :], "tm", 1)
    cot_next = passed_along(cotangent[:, :2], "tm", -1)
    both = jnp.concatenate(
        [jnp.concatenate([acts_past, acts], axis=1), jnp.concatenate([cotangent, cot_next], axis=1)]
    )
    both = padded(both, (("height", 2),), 1)
    acts_wide = both[: inputs.shape[0]]
    cot_wide = both[inputs.shape[0] :]
    acts_taps = row_patches(acts_wide)
    hidden = conv_rows(acts_taps, weight_one, inputs.shape) + bias_one
    gated = norm_act(hidden, gain_two)
    cot_taps = row_patches(cot_wide, (2, 1, 0))
    grad_gated = conv_rows(cot_taps, mirrored(weight_two), inputs.shape)
    flat_two = kernel_grad_reversed(gated, cot_taps)
    _, pull_norm_two = jax.vjp(norm_act, hidden, gain_two)
    grad_hidden, gain_two_part = pull_norm_two(grad_gated)
    grad_next = passed_along(grad_hidden[:, :2], "tm", -1)
    grad_wide = padded(jnp.concatenate([grad_hidden, grad_next], axis=1), (("height", 2),), 1)
    grad_acts = conv_rows(row_patches(grad_wide, (2, 1, 0)), mirrored(weight_one), inputs.shape)
    flat_one = kernel_grad_forward(acts_taps, grad_hidden)
    _, pull_norm_one = jax.vjp(norm_act, inputs, gain_one)
    grad_part, gain_one_part = pull_norm_one(grad_acts)
    grad_inputs = cotangent + grad_part
    channels = flat_one.shape[1]
    taps = flat_one.shape[0]
    count = (
        inputs.shape[0]
        * frames
        * rows
        * inputs.shape[3]
        * lax.axis_size("tm")
        * lax.axis_size("height")
        * lax.axis_size("batch")
    )
    factor = 1.0 / math.sqrt(count)
    parts = lax.axis_size("tm")
    share = taps // parts
    vectors = jnp.stack(
        [
            jnp.sum(grad_hidden, axis=(0, 1, 2, 3)),
            jnp.sum(cotangent, axis=(0, 1, 2, 3)),
            gain_one_part,
            gain_two_part,
        ]
    )
    packed = jnp.concatenate(
        [
            flat_one.reshape(parts, share, channels),
            flat_two.reshape(parts, share, channels),
            jnp.broadcast_to(vectors, (parts,) + vectors.shape),
        ],
        axis=1,
    )
    total = reduced(packed * factor)
    return (grad_inputs, total[:share], total[share : 2 * share], total[2 * share :])


def solution(mesh):
    placed = (
        P("batch", "tm", "height", None, None),
        P(),
        P(),
        P(),
        P(),
        P(),
        P("batch", "tm", "height", None, None),
    )
    return jax.shard_map(
        on_device,
        mesh=mesh,
        in_specs=placed,
        out_specs=(P("batch", "tm", "height", None, None), P("tm", None), P("tm", None), P()),
        check_vma=False,
    )
```

```python
import math

import jax
import jax.numpy as jnp
from jax import lax
from jax.sharding import PartitionSpec as P


def passed_along(block, axis, distance):
    devices = range(lax.axis_size(axis))
    route = [(i - distance, i) for i in devices if i - distance in devices]
    return lax.ppermute(block, axis, route)


def padded(block, sides, width):
    for axis, dim in sides:
        count = lax.axis_size(axis)
        top = lax.slice_in_dim(block, block.shape[dim] - width, None, axis=dim)
        bottom = lax.slice_in_dim(block, 0, width, axis=dim)
        if count == 2:
            first = lax.axis_index(axis) == 0
            got = lax.ppermute(jnp.where(first, top, bottom), axis, [(0, 1), (1, 0)])
            empty = jnp.zeros_like(got)
            low = jnp.where(first, empty, got)
            high = jnp.where(first, got, empty)
        else:
            forward = [(i, i + 1) for i in range(count - 1)]
            backward = [(target, source) for source, target in forward]
            low = lax.ppermute(top, axis, forward)
            high = lax.ppermute(bottom, axis, backward)
        block = jnp.concatenate([low, block, high], axis=dim)
    return block


def norm_act(values, scales):
    square = jnp.mean(values * values, axis=-1, keepdims=True)
    return jax.nn.silu(values * lax.rsqrt(square + 1e-06) * scales)


def row_patches(wide, order=(0, 1, 2)):
    frames = wide.shape[1] - 2
    rows = wide.shape[2] - 2
    extra = -(wide.shape[3] + 2) % 8
    edged = jnp.pad(wide, ((0, 0), (0, 0), (0, 0), (1, 1 + extra), (0, 0)))
    pieces = [edged[:, i : i + frames, j : j + rows] for i in order for j in order]
    taps = jnp.concatenate(pieces, axis=-1)
    return taps.reshape(-1, taps.shape[-1])


def conv_rows(taps, kernel, shape):
    cols = shape[3]
    width = kernel.shape[-1]
    stacked = jnp.transpose(kernel, (0, 1, 3, 2, 4)).reshape(-1, 3 * width)
    out = jnp.dot(taps, stacked, precision=lax.Precision.HIGH)
    out = out.reshape(tuple(shape[:3]) + (-1, 3 * width))
    return sum(out[:, :, :, l : l + cols, l * width : (l + 1) * width] for l in range(3))


def shifted_columns(values, order=(0, 1, 2)):
    extra = -(values.shape[3] + 2) % 8
    return jnp.concatenate(
        [jnp.pad(values, ((0, 0), (0, 0), (0, 0), (l, 2 - l + extra), (0, 0))) for l in order], axis=-1
    )


def kernel_grad_rows(taps, grad, order=(0, 1, 2)):
    width = grad.shape[-1]
    flat = lax.optimization_barrier(shifted_columns(grad, order).reshape(-1, 3 * width).T)
    spread = jnp.dot(flat, taps, precision=lax.Precision.HIGH)
    spread = spread.reshape(3, width, 3, 3, -1)
    return spread, width


def kernel_grad_forward(taps, grad):
    spread, width = kernel_grad_rows(taps, grad)
    return jnp.transpose(spread, (2, 3, 0, 4, 1)).reshape(-1, width)


def kernel_grad_reversed(values, taps):
    spread, channels = kernel_grad_rows(taps, values, (2, 1, 0))
    return jnp.transpose(spread, (2, 3, 0, 1, 4)).reshape(27 * channels, -1)


def mirrored(kernel):
    return jnp.swapaxes(kernel[:, :, ::-1], 3, 4)


def exchanged(block, axis, bit):
    count = lax.axis_size(axis)
    return lax.ppermute(block, axis, [(i, i ^ bit) for i in range(count)])


def halved(blocks, axis):
    count = lax.axis_size(axis)
    if count & (count - 1):
        return lax.psum_scatter(blocks, axis, scatter_dimension=0)
    me = lax.axis_index(axis)
    bit = 1
    while bit < count:
        mine = (me // bit) % 2
        pairs = blocks.reshape((blocks.shape[0] // 2, 2) + blocks.shape[1:])
        keep = lax.dynamic_index_in_dim(pairs, mine, axis=1, keepdims=False)
        send = lax.dynamic_index_in_dim(pairs, 1 - mine, axis=1, keepdims=False)
        blocks = keep + exchanged(send, axis, bit)
        bit *= 2
    return blocks[0]


def swapped_low(t):
    return t - t % 4 + (t % 2) * 2 + (t // 2) % 2


def halved_across(blocks):
    count = lax.axis_size("tm")
    heights = lax.axis_size("height")
    if count & (count - 1) or count < 4 or heights < 2:
        return halved(blocks, "tm")
    odd = lax.axis_index("height") % 2 == 1
    order = [swapped_low(k) for k in range(count)]
    blocks = jnp.where(odd, jnp.stack([blocks[k] for k in order]), blocks)
    me = lax.axis_index("tm")
    label = jnp.where(odd, swapped_low(me), me)
    bit = 1
    while bit < count:
        mine = (label // bit) % 2
        pairs = blocks.reshape((blocks.shape[0] // 2, 2) + blocks.shape[1:])
        keep = lax.dynamic_index_in_dim(pairs, mine, axis=1, keepdims=False)
        send = lax.dynamic_index_in_dim(pairs, 1 - mine, axis=1, keepdims=False)
        route = []
        for t in range(count):
            for h in range(heights):
                relabel = swapped_low if h % 2 else (lambda v: v)
                route.append((t * heights + h, relabel(relabel(t) ^ bit) * heights + h))
        blocks = keep + lax.ppermute(send, ("tm", "height"), route)
        bit *= 2
    return blocks[0]


def summed(block, axis):
    count = lax.axis_size(axis)
    if count & (count - 1):
        return lax.psum(block, axis)
    bit = 1
    while bit < count:
        block = block + exchanged(block, axis, bit)
        bit *= 2
    return block


def gathered(block, axis):
    count = lax.axis_size(axis)
    if count & (count - 1):
        return lax.all_gather(block, axis, tiled=True)
    me = lax.axis_index(axis)
    bit = 1
    while bit < count:
        other = exchanged(block, axis, bit)
        low = (me // bit) % 2 == 0
        block = jnp.where(low, jnp.concatenate([block, other]), jnp.concatenate([other, block]))
        bit *= 2
    return block


def reduced(blocks):
    parts, size, channels = blocks.shape
    split = lax.axis_size("height")
    width = -(-size // split)
    blocks = jnp.pad(blocks, ((0, 0), (0, width * split - size), (0, 0)))
    blocks = jnp.swapaxes(blocks.reshape(parts, split, width, channels), 0, 1)
    block = halved_across(halved(blocks, "height"))
    return gathered(summed(block, "batch"), "height")[:size]


def on_device(inputs, weight_one, bias_one, gain_one, weight_two, gain_two, cotangent):
    frames = inputs.shape[1]
    rows = inputs.shape[2]
    acts = norm_act(inputs, gain_one)
    acts_past = passed_along(acts[:, frames - 2 :], "tm", 1)
    cot_next = passed_along(cotangent[:, :2], "tm", -1)
    both = jnp.concatenate(
        [jnp.concatenate([acts_past, acts], axis=1), jnp.concatenate([cotangent, cot_next], axis=1)]
    )
    both = padded(both, (("height", 2),), 1)
    acts_wide = both[: inputs.shape[0]]
    cot_wide = both[inputs.shape[0] :]
    acts_taps = row_patches(acts_wide)
    hidden = conv_rows(acts_taps, weight_one, inputs.shape) + bias_one
    gated = norm_act(hidden, gain_two)
    cot_taps = row_patches(cot_wide, (2, 1, 0))
    grad_gated = conv_rows(cot_taps, mirrored(weight_two), inputs.shape)
    flat_two = kernel_grad_reversed(gated, cot_taps)
    _, pull_norm_two = jax.vjp(norm_act, hidden, gain_two)
    grad_hidden, gain_two_part = pull_norm_two(grad_gated)
    grad_next = passed_along(grad_hidden[:, :2], "tm", -1)
    grad_wide = padded(jnp.concatenate([grad_hidden, grad_next], axis=1), (("height", 2),), 1)
    grad_acts = conv_rows(row_patches(grad_wide, (2, 1, 0)), mirrored(weight_one), inputs.shape)
    flat_one = kernel_grad_forward(acts_taps, grad_hidden)
    _, pull_norm_one = jax.vjp(norm_act, inputs, gain_one)
    grad_part, gain_one_part = pull_norm_one(grad_acts)
    grad_inputs = cotangent + grad_part
    channels = flat_one.shape[1]
    taps = flat_one.shape[0]
    count = (
        inputs.shape[0]
        * frames
        * rows
        * inputs.shape[3]
        * lax.axis_size("tm")
        * lax.axis_size("height")
        * lax.axis_size("batch")
    )
    factor = 1.0 / math.sqrt(count)
    parts = lax.axis_size("tm")
    share = taps // parts
    vectors = jnp.stack(
        [
            jnp.sum(grad_hidden, axis=(0, 1, 2, 3)),
            jnp.sum(cotangent, axis=(0, 1, 2, 3)),
            gain_one_part,
            gain_two_part,
        ]
    )
    packed = jnp.concatenate(
        [
            flat_one.reshape(parts, share, channels),
            flat_two.reshape(parts, share, channels),
            jnp.broadcast_to(vectors, (parts,) + vectors.shape),
        ],
        axis=1,
    )
    total = reduced(packed * factor)
    return (grad_inputs, total[:share], total[share : 2 * share], total[2 * share :])


def solution(mesh):
    placed = (
        P("batch", "tm", "height", None, None),
        P(),
        P(),
        P(),
        P(),
        P(),
        P("batch", "tm", "height", None, None),
    )
    return jax.shard_map(
        on_device,
        mesh=mesh,
        in_specs=placed,
        out_specs=(P("batch", "tm", "height", None, None), P("tm", None), P("tm", None), P()),
        check_vma=False,
    )
```
